32 devices in a mesh: expert: 16 (over z, y, core), dp: 2 (over x).
Axes of the slice: x: 2, y: 2, z: 4, core: 2. Of those that a mesh axis runs over, the one named last changes fastest.
Arguments:
- tokens: bfloat16 [4096, 2048], P(('expert', 'dp')), may hold values from -6 to 6
- cotangent: bfloat16 [4096, 2048], P(('expert', 'dp')), may hold values from -6 to 6
- expert_ids: int32 [4096, 6], P(('expert', 'dp')), may hold values from 0 to 15, all different within a row; in each aligned block of 128 rows (0 to 127, 128 to 255, ...) at most 60 rows name the same one
- gate_vals: float32 [4096, 6], P(('expert', 'dp')), may hold values from 0.05 to 0.5
- capacity: int32 [16], replicated, may hold values from 384 to 960
- w_gate: bfloat16 [16, 384, 2048], P('expert', 'dp'), may hold values from -0.125 to 0.125
- w_up: bfloat16 [16, 384, 2048], P('expert', 'dp'), may hold values from -0.125 to 0.125
- w_down: bfloat16 [16, 384, 2048], P('expert', 'dp'), may hold values from -0.3125 to 0.3125
Outputs:
- layer_out: bfloat16 [4096, 2048], P(('expert', 'dp'))
- grad_tokens: bfloat16 [4096, 2048], P(('expert', 'dp'))
- grad_gates: float32 [4096, 6], P(('expert', 'dp'))
- grad_gate_w: bfloat16 [16, 384, 2048], P('expert', 'dp')
- grad_up_w: bfloat16 [16, 384, 2048], P('expert', 'dp')
- grad_down_w: bfloat16 [16, 384, 2048], P('expert', 'dp')
The draws below stay inside these ranges and needn't reach their ends.
Inputs may be any that keep to these rules, and one draw needn't show every extreme that they name: `expert_ids`: within the 128 rows of one device no expert is named more than 60 times, a bound that some block reaches.
All inputs are finite; a program needn't handle non-finite values.
Results may differ from the reference program's by a relative error of at most 0.0065.
Values may be sent and summed in bfloat16 or wider, within the bound.
No kernel may reach another device: no remote copies, remote signals or barrier semaphores. Data moves between devices by JAX's collectives and lax.ppermute only.
A program may use at most 128 MiB of HBM per device.

```python
import math
import jax
import jax.numpy as jnp
import numpy as np
from jax import lax

D = 2048
FF = 384
TOP = 6
TOK_DEV = 128
EXPERTS = 16
TOKENS = 4096
CAP = 60
CAP_LO = 384
CAP_HI = 960
N_EXPERT = 16
N_DP = 2


def draw_capacity(key, part):
    first_key, second_key = jax.random.split(key, 2)
    values = jax.random.randint(first_key, (EXPERTS,), CAP_LO, CAP_HI + 1)
    order = jax.random.permutation(second_key, EXPERTS)
    values = values.at[order[0]].set(CAP_HI)
    values = values.at[order[1]].set(CAP_LO)
    return values.astype(jnp.int32)


def steps_of(own_key, extent, cuts, smallest, largest):
    factor_of = 1.0
    for axis_at, shards_of in cuts:
        heights = jax.random.uniform(jax.random.fold_in(jax.random.fold_in(own_key, 6), axis_at), (shards_of,), jnp.float32, smallest / len(cuts), largest / len(cuts))
        factor_of = factor_of * jnp.repeat(jnp.exp(heights), extent[axis_at] // shards_of).reshape((-1,) + (1,) * (len(extent) - 1 - axis_at))
    return factor_of


def assign_block(own_key, own, number, rows, number_of, top, bound, skew):
    sequence = jax.random.permutation(own_key, number_of)
    heavy_load, common = load_shares(number_of, rows * top, bound, skew, True), load_shares(number_of, rows * top, bound, skew, False)
    places = jnp.arange(number_of)

    def named(tallies, turn):
        used = int((tallies > 0).sum())
        fixed = max(1, used // 4)
        passed = fixed + (places - fixed + turn * (used - fixed)) % max(1, number_of - fixed)
        return jnp.zeros((number_of,), jnp.int32).at[sequence[jnp.where(places < fixed, places, passed)]].set(jnp.asarray(tallies, jnp.int32))

    tallies = jnp.where(number % 4 == 0, named(heavy_load, number // 4), named(common, number - number // 4 - 1))
    mixed = jax.random.permutation(jax.random.fold_in(own, 3), number_of)
    source_of, receiver = mixed[0:number_of // 2 * 2:2], mixed[1:number_of // 2 * 2:2]
    slack = jnp.minimum(tallies[source_of] - 1, bound - tallies[receiver]) // 2
    slack = jnp.where((source_of == sequence[0]) | (receiver == sequence[0]) | (tallies[receiver] == 0), 0, jnp.maximum(slack, 0))
    passed = jax.random.randint(jax.random.fold_in(own, 4), (number_of // 2,), 0, 1 << 20) % (slack + 1)
    tallies = tallies.at[source_of].add(-passed).at[receiver].add(passed)
    labels = jnp.searchsorted(jnp.cumsum(tallies), jnp.arange(rows * top), side="right").astype(jnp.int32)
    grid = labels.reshape(top, rows).T
    grid = grid[jax.random.permutation(jax.random.fold_in(own, 1), rows)]
    turn = jax.random.randint(jax.random.fold_in(own, 2), (rows, 1), 0, top)
    return jnp.take_along_axis(grid, (jnp.arange(top)[None, :] + turn) % top, axis=1)


def load_shares(count, total, limit, skew, full):
    portions = [(1 << 20) // math.isqrt(grade ** skew) + 1 for grade in range(1, count + 1)]
    largest = limit if full else min(limit, max(-(-total // count), total * portions[0] // sum(portions)))
    least = 1 if total - largest >= count - 1 else 0
    holding, spare = [largest] + [least] * (count - 1), total - largest - least * (count - 1)
    while spare > 0:
        movable = [i for i in range(1, count) if holding[i] < largest] or [i for i in range(1, count) if holding[i] < limit]
        whole, remaining = sum([portions[i] for i in movable]), spare
        for i in movable:
            more = min(limit - holding[i], max(1, remaining * portions[i] // whole), spare)
            holding[i] = holding[i] + more
            spare = spare - more
    return np.array(holding)


def noise(stream_key, shape, scale, limit, cuts=(), kind=jnp.bfloat16):
    drawn = scale * jax.random.normal(stream_key, shape, jnp.float32)
    if cuts:
        drawn = drawn * steps_of(stream_key, shape, cuts, -0.22, 0.18)
    return jnp.clip(drawn, -limit, limit).astype(kind)


def setup_inputs(seed: int = 0) -> dict:
    key_of = jax.random.split(jax.random.key(seed), 9)
    tokens = noise(key_of[0], (TOKENS, D), 1.0, 6.0, ((0, 32),))
    cotangent = noise(key_of[1], (TOKENS, D), 1.0, 6.0, ((0, 32),))
    expert_ids_keys = jax.random.split(jax.random.fold_in(key_of[2], 1), TOKENS // TOK_DEV)
    expert_ids_turns = jax.random.permutation(jax.random.fold_in(key_of[2], 3), TOKENS // TOK_DEV)
    expert_ids = jax.vmap(lambda own, number: assign_block(jax.random.fold_in(key_of[2], 2), own, number, TOK_DEV, EXPERTS, TOP, CAP, 2))(expert_ids_keys, expert_ids_turns).reshape((TOKENS, TOP))
    gate_vals = jnp.clip(0.05 + 0.45 * jax.random.uniform(key_of[3], (TOKENS, TOP), jnp.float32) ** steps_of(key_of[3], (TOKENS, TOP), ((0, 32),), -0.2, 0.2), 0.05, 0.5)
    capacity = draw_capacity(jax.random.fold_in(key_of[8], 71), 0)
    w_gate = noise(key_of[5], (EXPERTS, FF, D), D ** -0.5, 0.125, ((0, 16), (1, 2)))
    w_up = noise(key_of[6], (EXPERTS, FF, D), D ** -0.5, 0.125, ((0, 16), (1, 2)))
    w_down = noise(key_of[7], (EXPERTS, FF, D), FF ** -0.5, 0.3125, ((0, 16), (1, 2)))
    return {"tokens": tokens, "cotangent": cotangent, "expert_ids": expert_ids, "gate_vals": gate_vals, "capacity": capacity, "w_gate": w_gate, "w_up": w_up, "w_down": w_down}


def one_expert(operands):
    rows_in, rows_cot, gate_mat, up_mat, down_mat = operands
    gate_pre = jnp.dot(rows_in, gate_mat.T, preferred_element_type=jnp.float32)
    up_pre = jnp.dot(rows_in, up_mat.T, preferred_element_type=jnp.float32)
    sigmoid_gate = jax.nn.sigmoid(gate_pre)
    activated = gate_pre * sigmoid_gate
    hidden = (activated * up_pre).astype(jnp.bfloat16)
    d_hidden = jnp.dot(rows_cot, down_mat.T, preferred_element_type=jnp.float32)
    d_gate = (d_hidden * up_pre * (sigmoid_gate + activated * (1.0 - sigmoid_gate))).astype(jnp.bfloat16)
    d_up = (d_hidden * activated).astype(jnp.bfloat16)
    out_rows = jnp.dot(hidden, down_mat, preferred_element_type=jnp.float32).astype(jnp.bfloat16)
    back = jnp.dot(d_gate, gate_mat, preferred_element_type=jnp.float32)
    back = back + jnp.dot(d_up, up_mat, preferred_element_type=jnp.float32)
    grad_down = jnp.dot(hidden.T, rows_cot, preferred_element_type=jnp.float32).astype(jnp.bfloat16)
    grad_gate = jnp.dot(d_gate.T, rows_in, preferred_element_type=jnp.float32).astype(jnp.bfloat16)
    grad_up = jnp.dot(d_up.T, rows_in, preferred_element_type=jnp.float32).astype(jnp.bfloat16)
    return out_rows, back.astype(jnp.bfloat16), grad_gate, grad_up, grad_down


def reference(tokens, cotangent, expert_ids, gate_vals, capacity, w_gate, w_up, w_down):
    per_device = TOK_DEV * TOP
    route_ids = expert_ids.reshape(N_EXPERT, N_DP, per_device)
    one_hot = (route_ids[..., None] == jnp.arange(EXPERTS, dtype=jnp.int32)).astype(jnp.int32)
    running = jnp.cumsum(one_hot, axis=2)
    local_rank = jnp.sum(running * one_hot, axis=-1) - 1
    counts = running[:, :, -1, :]
    earlier = jnp.cumsum(counts, axis=0) - counts
    offset = jnp.sum(one_hot * earlier[:, :, None, :], axis=-1)
    kept = (offset + local_rank) < capacity[route_ids]
    slots_all = N_DP * N_EXPERT * CAP
    device = jnp.arange(N_EXPERT, dtype=jnp.int32)[:, None, None]
    replica = jnp.arange(N_DP, dtype=jnp.int32)[None, :, None]
    position = route_ids * slots_all + replica * (N_EXPERT * CAP) + device * CAP + local_rank
    position = jnp.where(kept, position, EXPERTS * slots_all).astype(jnp.int32).reshape(-1)
    input_routes = jnp.repeat(tokens, TOP, axis=0)
    cot_routes = (gate_vals.reshape(-1)[:, None] * jnp.repeat(cotangent, TOP, axis=0).astype(jnp.float32)).astype(jnp.bfloat16)
    input_buf = jnp.zeros((EXPERTS * slots_all, D), jnp.bfloat16).at[position].set(input_routes, mode="drop")
    cot_buf = jnp.zeros((EXPERTS * slots_all, D), jnp.bfloat16).at[position].set(cot_routes, mode="drop")
    input_buf = input_buf.reshape(EXPERTS, slots_all, D)
    cot_buf = cot_buf.reshape(EXPERTS, slots_all, D)
    expert_out, expert_dx, grad_gate_w, grad_up_w, grad_down_w = lax.map(one_expert, (input_buf, cot_buf, w_gate, w_up, w_down))
    picked_out = jnp.take(expert_out.reshape(-1, D), position, axis=0, mode="fill", fill_value=0)
    picked_dx = jnp.take(expert_dx.reshape(-1, D), position, axis=0, mode="fill", fill_value=0)
    picked_out = picked_out.reshape(TOKENS, TOP, D).astype(jnp.float32)
    picked_dx = picked_dx.reshape(TOKENS, TOP, D).astype(jnp.float32)
    layer_out = jnp.sum(gate_vals[:, :, None] * picked_out, axis=1).astype(jnp.bfloat16)
    grad_tokens = jnp.sum(picked_dx, axis=1).astype(jnp.bfloat16)
    grad_gates = jnp.sum(cotangent.astype(jnp.float32)[:, None, :] * picked_out, axis=-1)
    return layer_out, grad_tokens, grad_gates, grad_gate_w, grad_up_w, grad_down_w
```

```python
import jax
import jax.numpy as jnp
import numpy as np
from jax import lax
from jax.sharding import Mesh
from jax.sharding import PartitionSpec as P


def shifted(value, axis, count, shift):
    return lax.ppermute(value, axis, [(j, (j + shift) % count) for j in range(count)])


def on_device(tokens, cotangent, expert_ids, gate_vals, capacity, w_gate, w_up, w_down):
    tok_rows, width = tokens.shape
    top_count = expert_ids.shape[1]
    experts = capacity.shape[0]
    local_experts, hidden_part, _ = w_gate.shape
    slots = max(2, (5 * tok_rows * top_count + 4 * experts - 1) // (4 * experts))
    n_in = lax.axis_size("inner")
    n_dp = lax.axis_size("dp")
    half = lax.axis_index("half")
    source = half * n_in + lax.axis_index("inner")
    n_src = 2 * n_in
    half_experts = n_in * local_experts
    half_rows = half_experts * slots

    both_rows = jnp.concatenate([tokens, cotangent], axis=1)
    partner_rows = shifted(both_rows, "half", 2, 1)
    partner_gates = shifted(gate_vals, "half", 2, 1)

    weights = jnp.concatenate([w_gate, w_up, w_down], axis=0)
    pieces = [weights] + [shifted(weights, "dp", n_dp, d) for d in range(1, n_dp)]
    full = jnp.concatenate(pieces, axis=1)
    full_gate = full[:local_experts]
    full_up = full[local_experts : 2 * local_experts]
    full_down = full[2 * local_experts :]

    flat_ids = expert_ids.reshape(-1)
    one_hot = (flat_ids[:, None] == jnp.arange(experts, dtype=jnp.int32)[None, :]).astype(jnp.int32)
    running = jnp.cumsum(one_hot, axis=0)
    local_rank = jnp.sum(running * one_hot, axis=1) - 1
    counts = running[-1]
    all_counts = lax.all_gather(counts, ("half", "inner"))
    lower = jnp.arange(n_src, dtype=jnp.int32)[:, None] < source
    earlier = jnp.sum(jnp.where(lower, all_counts, 0), axis=0)
    offset = jnp.sum(one_hot * earlier[None, :], axis=1)
    limit = jnp.sum(one_hot * capacity[None, :], axis=1)
    kept = offset + local_rank < limit
    code = jnp.where(kept, flat_ids * slots + local_rank, -1).reshape(tok_rows, top_count)
    partner_code = shifted(code, "half", 2, 1)

    def place(codes):
        local = codes // slots - half * half_experts
        inside = (codes >= 0) & (local >= 0) & (local < half_experts)
        return jnp.where(inside, local * slots + codes % slots, -1)

    own_place = place(code)
    partner_place = place(partner_code)

    all_rows = jnp.stack([both_rows, partner_rows])
    all_gates = jnp.stack([gate_vals, partner_gates])
    all_place = jnp.stack([own_place, partner_place])
    x_routes = jnp.broadcast_to(all_rows[:, :, None, :width], (2, tok_rows, top_count, width))
    c_routes = (
        all_gates[:, :, :, None] * all_rows[:, :, None, width:].astype(jnp.float32)
    ).astype(jnp.bfloat16)
    routes = jnp.concatenate([x_routes, c_routes], axis=-1).reshape(-1, 2 * width)
    side = jnp.arange(2, dtype=jnp.int32)[:, None, None]
    dest = jnp.where(
        all_place >= 0,
        (all_place // slots * 2 + side) * slots + all_place % slots,
        2 * half_rows,
    ).reshape(-1)
    send = jnp.zeros((2 * half_rows, 2 * width), jnp.bfloat16).at[dest].set(routes, mode="drop")
    send = send.reshape(half_experts, 2 * slots, 2 * width)
    got = lax.all_to_all(send, "inner", split_axis=0, concat_axis=0, tiled=True)
    got = got.reshape(n_in, local_experts, 2 * slots, 2 * width).transpose(1, 0, 2, 3)
    got = got.reshape(local_experts, n_in * 2 * slots, 2 * width)
    rows_in = got[:, :, :width]
    rows_cot = got[:, :, width:]

    gate_pre = jnp.einsum("erd,efd->erf", rows_in, full_gate, preferred_element_type=jnp.float32)
    up_pre = jnp.einsum("erd,efd->erf", rows_in, full_up, preferred_element_type=jnp.float32)
    sigmoid_gate = jax.nn.sigmoid(gate_pre)
    activated = gate_pre * sigmoid_gate
    hidden = (activated * up_pre).astype(jnp.bfloat16)
    out_rows = jnp.einsum(
        "erf,efd->erd", hidden, full_down, preferred_element_type=jnp.float32
    ).astype(jnp.bfloat16)
    d_hidden = jnp.einsum("erd,efd->erf", rows_cot, full_down, preferred_element_type=jnp.float32)
    d_gate = (d_hidden * up_pre * (sigmoid_gate + activated * (1.0 - sigmoid_gate))).astype(
        jnp.bfloat16
    )
    d_up = (d_hidden * activated).astype(jnp.bfloat16)
    dx_rows = jnp.einsum("erf,efd->erd", d_gate, full_gate, preferred_element_type=jnp.float32)
    dx_rows = (
        dx_rows + jnp.einsum("erf,efd->erd", d_up, full_up, preferred_element_type=jnp.float32)
    ).astype(jnp.bfloat16)
    part_down = jnp.einsum("erf,erd->efd", hidden, rows_cot, preferred_element_type=jnp.float32)
    part_gate = jnp.einsum("erf,erd->efd", d_gate, rows_in, preferred_element_type=jnp.float32)
    part_up = jnp.einsum("erf,erd->efd", d_up, rows_in, preferred_element_type=jnp.float32)

    back = jnp.concatenate([out_rows, dx_rows], axis=-1)
    back = back.reshape(local_experts, n_in, 2 * slots, 2 * width).transpose(1, 0, 2, 3)
    back = back.reshape(half_experts, 2 * slots, 2 * width)
    back = lax.all_to_all(back, "inner", split_axis=0, concat_axis=0, tiled=True)
    back = back.reshape(half_experts, 2, slots, 2 * width)

    parts = jnp.concatenate([part_gate, part_up, part_down], axis=0)
    summed = parts[:, :hidden_part]
    for d in range(1, n_dp):
        block = parts[:, d * hidden_part : (d + 1) * hidden_part].astype(jnp.bfloat16)
        summed = summed + shifted(block, "dp", n_dp, -d).astype(jnp.float32)
    summed = summed.astype(jnp.bfloat16)
    grad_gate_w = summed[:local_experts]
    grad_up_w = summed[local_experts : 2 * local_experts]
    grad_down_w = summed[2 * local_experts :]

    columns = jnp.arange(half_rows, dtype=jnp.int32)

    def combine(which):
        rows = back[:, which].reshape(half_rows, 2 * width)
        out_part = rows[:, :width]
        dx_part = rows[:, width:]
        hit = all_place[which][:, :, None] == columns[None, None, :]
        weight = jnp.sum(jnp.where(hit, all_gates[which][:, :, None], 0.0), axis=1)
        ones = jnp.sum(hit.astype(jnp.float32), axis=1).astype(jnp.bfloat16)
        layer = jnp.dot(
            weight, out_part.astype(jnp.float32), precision=lax.Precision.HIGHEST,
            preferred_element_type=jnp.float32,
        )
        grads = jnp.dot(ones, dx_part, preferred_element_type=jnp.float32)
        scores = jnp.dot(
            all_rows[which][:, width:], out_part.T, preferred_element_type=jnp.float32
        )
        gates = jnp.sum(jnp.where(hit, scores[:, None, :], 0.0), axis=2)
        return layer, grads, gates

    partner_layer, partner_grads, partner_gg = combine(1)
    returned = shifted(
        jnp.concatenate([partner_layer, partner_grads], axis=1).astype(jnp.bfloat16), "half", 2, 1
    )
    returned_gg = shifted(partner_gg, "half", 2, 1)
    own_layer, own_grads, own_gg = combine(0)
    layer_out = (own_layer + returned[:, :width].astype(jnp.float32)).astype(jnp.bfloat16)
    grad_tokens = (own_grads + returned[:, width:].astype(jnp.float32)).astype(jnp.bfloat16)
    grad_gates = own_gg + returned_gg
    return (layer_out, grad_tokens, grad_gates, grad_gate_w, grad_up_w, grad_down_w)


def solution(mesh):
    n_expert = mesh.shape["expert"]
    n_dp = mesh.shape["dp"]
    devices = np.asarray(mesh.devices).reshape(2, n_expert // 2, n_dp)
    split = Mesh(devices, ("half", "inner", "dp"))
    rows = P(("half", "inner", "dp"), None)
    weights = P(("half", "inner"), "dp", None)
    return jax.shard_map(
        on_device,
        mesh=split,
        in_specs=(rows, rows, rows, rows, P(), weights, weights, weights),
        out_specs=(rows, rows, rows, weights, weights, weights),
        check_vma=False,
    )
```

```python
import jax
import jax.numpy as jnp
import numpy as np
from jax import lax
from jax.sharding import Mesh
from jax.sharding import PartitionSpec as P


def shifted(value, axis, count, shift):
    return lax.ppermute(value, axis, [(j, (j + shift) % count) for j in range(count)])


def in_three(value):
    first = value.astype(jnp.bfloat16)
    rest = value - first.astype(jnp.float32)
    second = rest.astype(jnp.bfloat16)
    third = (rest - second.astype(jnp.float32)).astype(jnp.bfloat16)
    return jnp.concatenate([first, second, third], axis=0)


def on_device(tokens, cotangent, expert_ids, gate_vals, capacity, w_gate, w_up, w_down):
    tok_rows, width = tokens.shape
    top_count = expert_ids.shape[1]
    experts = capacity.shape[0]
    local_experts, hidden_part, _ = w_gate.shape
    slots = max(2, (5 * tok_rows * top_count + 4 * experts - 1) // (4 * experts))
    n_in = lax.axis_size("inner")
    n_dp = lax.axis_size("dp")
    half = lax.axis_index("half")
    inner = lax.axis_index("inner")
    source = half * n_in + inner
    n_src = 2 * n_in
    half_experts = n_in * local_experts
    half_rows = half_experts * slots

    weights = jnp.concatenate([w_gate, w_up, w_down], axis=0)
    pieces = [weights] + [shifted(weights, "dp", n_dp, d) for d in range(1, n_dp)]

    both_rows = jnp.concatenate([tokens, cotangent], axis=1)
    partner_rows = shifted(both_rows, "half", 2, 1)
    partner_gates = shifted(gate_vals, "half", 2, 1)

    flat_ids = expert_ids.reshape(-1)
    one_hot = (flat_ids[:, None] == jnp.arange(experts, dtype=jnp.int32)[None, :]).astype(jnp.int32)
    running = jnp.cumsum(one_hot, axis=0)
    local_rank = jnp.sum(running * one_hot, axis=1) - 1
    counts = running[-1]
    count_rows = jnp.where(jnp.arange(n_src, dtype=jnp.int32)[:, None] == source, counts[None, :], 0)
    all_counts = lax.psum(count_rows, ("half", "inner"))
    code = (flat_ids * slots + local_rank).reshape(tok_rows, top_count)
    partner_code = shifted(code, "half", 2, 1)

    all_rows = jnp.concatenate([both_rows, partner_rows], axis=0)
    all_gates = jnp.concatenate([gate_vals, partner_gates], axis=0)
    all_code = jnp.concatenate([code, partner_code], axis=0)
    local = all_code // slots - half * half_experts
    inside = (local >= 0) & (local < half_experts)
    side = (jnp.arange(2 * tok_rows, dtype=jnp.int32) >= tok_rows).astype(jnp.int32)[:, None]
    dest = jnp.where(inside, (local * 2 + side) * slots + all_code % slots, 2 * half_rows)

    row_of = jnp.broadcast_to(jnp.arange(2 * tok_rows, dtype=jnp.int32)[:, None], dest.shape)
    filled_by = jnp.full((2 * half_rows,), -1, jnp.int32).at[dest.reshape(-1)].set(
        row_of.reshape(-1), mode="drop"
    )
    slot_gate = jnp.zeros((2 * half_rows,), jnp.float32).at[dest.reshape(-1)].set(
        all_gates.reshape(-1), mode="drop"
    )
    pick = (filled_by[:, None] == jnp.arange(2 * tok_rows, dtype=jnp.int32)[None, :]).astype(
        jnp.bfloat16
    )
    picked = jnp.dot(pick, all_rows, preferred_element_type=jnp.float32)
    send_x = picked[:, :width].astype(jnp.bfloat16)
    send_c = (slot_gate[:, None] * picked[:, width:]).astype(jnp.bfloat16)
    send = jnp.stack(
        [send_x.reshape(half_experts, 2 * slots, width), send_c.reshape(half_experts, 2 * slots, width)],
        axis=1,
    )
    got = lax.all_to_all(send, "inner", split_axis=0, concat_axis=0, tiled=True)
    got = got.reshape(n_in, local_experts, 2, 2, slots, width)

    earlier = jnp.cumsum(all_counts, axis=0) - all_counts
    holders = jnp.arange(n_in, dtype=jnp.int32)[:, None]
    halves = jnp.stack([half, 1 - half])[None, :]
    sources = halves * n_in + holders
    mine = (half * n_in + inner) * local_experts + jnp.arange(local_experts, dtype=jnp.int32)
    before = earlier[sources][:, :, mine].transpose(0, 2, 1)
    ranks = jnp.arange(slots, dtype=jnp.int32)
    keep = before[..., None] + ranks < capacity[mine][None, :, None, None]
    got = jnp.where(keep[:, :, None, :, :, None], got, jnp.zeros((), got.dtype))
    got = got.transpose(1, 2, 0, 3, 4, 5).reshape(local_experts, 2, n_in * 2 * slots, width)
    rows_in = got[:, 0]
    rows_cot = got[:, 1]

    full = jnp.concatenate(pieces, axis=1)
    full_gate = full[:local_experts]
    full_up = full[local_experts : 2 * local_experts]
    full_down = full[2 * local_experts :]

    gate_pre = jnp.einsum("erd,efd->erf", rows_in, full_gate, preferred_element_type=jnp.float32)
    up_pre = jnp.einsum("erd,efd->erf", rows_in, full_up, preferred_element_type=jnp.float32)
    sigmoid_gate = jax.nn.sigmoid(gate_pre)
    activated = gate_pre * sigmoid_gate
    hidden = (activated * up_pre).astype(jnp.bfloat16)
    out_rows = jnp.einsum(
        "erf,efd->erd", hidden, full_down, preferred_element_type=jnp.float32
    ).astype(jnp.bfloat16)
    d_hidden = jnp.einsum("erd,efd->erf", rows_cot, full_down, preferred_element_type=jnp.float32)
    d_gate = (d_hidden * up_pre * (sigmoid_gate + activated * (1.0 - sigmoid_gate))).astype(
        jnp.bfloat16
    )
    d_up = (d_hidden * activated).astype(jnp.bfloat16)
    dx_rows = jnp.einsum("erf,efd->erd", d_gate, full_gate, preferred_element_type=jnp.float32)
    dx_rows = (
        dx_rows + jnp.einsum("erf,efd->erd", d_up, full_up, preferred_element_type=jnp.float32)
    ).astype(jnp.bfloat16)
    part_down = jnp.einsum("erf,erd->efd", hidden, rows_cot, preferred_element_type=jnp.float32)
    part_gate = jnp.einsum("erf,erd->efd", d_gate, rows_in, preferred_element_type=jnp.float32)
    part_up = jnp.einsum("erf,erd->efd", d_up, rows_in, preferred_element_type=jnp.float32)

    back = jnp.stack([out_rows, dx_rows], axis=1)
    back = back.reshape(local_experts, 2, n_in, 2 * slots, width).transpose(2, 0, 1, 3, 4)
    back = back.reshape(half_experts, 2, 2 * slots, width)
    back = lax.all_to_all(back, "inner", split_axis=0, concat_axis=0, tiled=True)

    parts = jnp.concatenate([part_gate, part_up, part_down], axis=0)
    summed = parts[:, :hidden_part]
    for d in range(1, n_dp):
        block = parts[:, d * hidden_part : (d + 1) * hidden_part].astype(jnp.bfloat16)
        summed = summed + shifted(block, "dp", n_dp, -d).astype(jnp.float32)
    summed = summed.astype(jnp.bfloat16)
    grad_gate_w = summed[:local_experts]
    grad_up_w = summed[local_experts : 2 * local_experts]
    grad_down_w = summed[2 * local_experts :]

    out_part = back[:, 0].reshape(2 * half_rows, width)
    dx_part = back[:, 1].reshape(2 * half_rows, width)
    hit = dest[:, :, None] == jnp.arange(2 * half_rows, dtype=jnp.int32)[None, None, :]
    weight = jnp.sum(jnp.where(hit, all_gates[:, :, None], 0.0), axis=1)
    ones = jnp.sum(hit.astype(jnp.float32), axis=1).astype(jnp.bfloat16)
    layer = jnp.dot(in_three(weight), out_part, preferred_element_type=jnp.float32)
    n_all = 2 * tok_rows
    layer = layer[:n_all] + layer[n_all : 2 * n_all] + layer[2 * n_all :]
    grads = jnp.dot(ones, dx_part, preferred_element_type=jnp.float32)
    scores = jnp.dot(all_rows[:, width:], out_part.T, preferred_element_type=jnp.float32)
    gg = jnp.sum(jnp.where(hit, scores[:, None, :], 0.0), axis=2)

    returned = shifted(
        jnp.concatenate([layer[tok_rows:], grads[tok_rows:]], axis=1).astype(jnp.bfloat16),
        "half",
        2,
        1,
    )
    returned_gg = shifted(gg[tok_rows:], "half", 2, 1)
    layer_out = (layer[:tok_rows] + returned[:, :width].astype(jnp.float32)).astype(jnp.bfloat16)
    grad_tokens = (grads[:tok_rows] + returned[:, width:].astype(jnp.float32)).astype(jnp.bfloat16)
    grad_gates = gg[:tok_rows] + returned_gg
    return (layer_out, grad_tokens, grad_gates, grad_gate_w, grad_up_w, grad_down_w)


def solution(mesh):
    n_expert = mesh.shape["expert"]
    n_dp = mesh.shape["dp"]
    devices = np.asarray(mesh.devices).reshape(2, n_expert // 2, n_dp)
    split = Mesh(devices, ("half", "inner", "dp"))
    rows = P(("half", "inner", "dp"), None)
    weights = P(("half", "inner"), "dp", None)
    return jax.shard_map(
        on_device,
        mesh=split,
        in_specs=(rows, rows, rows, rows, P(), weights, weights, weights),
        out_specs=(rows, rows, rows, weights, weights, weights),
        check_vma=False,
    )
```

```python
import jax
import jax.numpy as jnp
import numpy as np
from jax import lax
from jax.sharding import Mesh
from jax.sharding import PartitionSpec as P


def shifted(value, axis, count, shift):
    return lax.ppermute(value, axis, [(j, (j + shift) % count) for j in range(count)])


def in_three(value):
    first = value.astype(jnp.bfloat16)
    rest = value - first.astype(jnp.float32)
    second = rest.astype(jnp.bfloat16)
    third = (rest - second.astype(jnp.float32)).astype(jnp.bfloat16)
    return jnp.concatenate([first, second, third], axis=0)


def on_device(tokens, cotangent, expert_ids, gate_vals, capacity, w_gate, w_up, w_down):
    tok_rows, width = tokens.shape
    top_count = expert_ids.shape[1]
    experts = capacity.shape[0]
    local_experts, hidden_part, _ = w_gate.shape
    slots = max(2, (5 * tok_rows * top_count + 4 * experts - 1) // (4 * experts))
    n_in = lax.axis_size("inner")
    n_dp = lax.axis_size("dp")
    half = lax.axis_index("half")
    inner = lax.axis_index("inner")
    source = half * n_in + inner
    n_src = 2 * n_in
    half_experts = n_in * local_experts
    half_rows = half_experts * slots

    weights = jnp.concatenate([w_gate, w_up, w_down], axis=0)
    pieces = [weights] + [shifted(weights, "dp", n_dp, d) for d in range(1, n_dp)]

    both_rows = jnp.concatenate([tokens, cotangent], axis=1)
    partner_rows = shifted(both_rows, "half", 2, 1)
    partner_gates = shifted(gate_vals, "half", 2, 1)

    flat_ids = expert_ids.reshape(-1)
    one_hot = (flat_ids[:, None] == jnp.arange(experts, dtype=jnp.int32)[None, :]).astype(jnp.int32)
    running = jnp.cumsum(one_hot, axis=0)
    local_rank = jnp.sum(running * one_hot, axis=1) - 1
    counts = running[-1]
    count_rows = jnp.where(jnp.arange(n_src, dtype=jnp.int32)[:, None] == source, counts[None, :], 0)
    all_counts = lax.psum(count_rows.astype(jnp.float32), ("half", "inner")).astype(jnp.int32)
    code = (flat_ids * slots + local_rank).reshape(tok_rows, top_count)
    partner_code = shifted(code, "half", 2, 1)

    all_rows = jnp.concatenate([both_rows, partner_rows], axis=0)
    all_gates = jnp.concatenate([gate_vals, partner_gates], axis=0)
    all_code = jnp.concatenate([code, partner_code], axis=0)
    local = all_code // slots - half * half_experts
    inside = (local >= 0) & (local < half_experts)
    side = (jnp.arange(2 * tok_rows, dtype=jnp.int32) >= tok_rows).astype(jnp.int32)[:, None]
    dest = jnp.where(inside, (local * 2 + side) * slots + all_code % slots, 2 * half_rows)

    row_of = jnp.broadcast_to(jnp.arange(2 * tok_rows, dtype=jnp.int32)[:, None], dest.shape)
    filled_by = jnp.full((2 * half_rows,), -1, jnp.int32).at[dest.reshape(-1)].set(
        row_of.reshape(-1), mode="drop"
    )
    slot_gate = jnp.zeros((2 * half_rows,), jnp.float32).at[dest.reshape(-1)].set(
        all_gates.reshape(-1), mode="drop"
    )
    pick = (filled_by[:, None] == jnp.arange(2 * tok_rows, dtype=jnp.int32)[None, :]).astype(
        jnp.bfloat16
    )
    picked = jnp.dot(pick, all_rows, preferred_element_type=jnp.float32)
    send_x = picked[:, :width].astype(jnp.bfloat16)
    send_c = (slot_gate[:, None] * picked[:, width:]).astype(jnp.bfloat16)
    send = jnp.concatenate([send_x, send_c], axis=1).reshape(half_experts, 2 * slots, 2 * width)
    got = lax.all_to_all(send, "inner", split_axis=0, concat_axis=0, tiled=True)
    got = got.reshape(n_in, local_experts, 2, slots, 2 * width)

    earlier = jnp.cumsum(all_counts, axis=0) - all_counts
    holders = jnp.arange(n_in, dtype=jnp.int32)[:, None]
    halves = jnp.stack([half, 1 - half])[None, :]
    sources = halves * n_in + holders
    mine = (half * n_in + inner) * local_experts + jnp.arange(local_experts, dtype=jnp.int32)
    before = earlier[sources][:, :, mine].transpose(0, 2, 1)
    ranks = jnp.arange(slots, dtype=jnp.int32)
    keep = before[..., None] + ranks < capacity[mine][None, :, None, None]
    got = jnp.where(keep[..., None], got, jnp.zeros((), got.dtype))
    got = got.transpose(1, 0, 2, 3, 4).reshape(local_experts, n_in * 2 * slots, 2 * width)
    rows_in = got[:, :, :width]
    rows_cot = got[:, :, width:]

    full = jnp.concatenate(pieces, axis=1)
    full_gate = full[:local_experts]
    full_up = full[local_experts : 2 * local_experts]
    full_down = full[2 * local_experts :]

    gate_pre = jnp.einsum("erd,efd->erf", rows_in, full_gate, preferred_element_type=jnp.float32)
    up_pre = jnp.einsum("erd,efd->erf", rows_in, full_up, preferred_element_type=jnp.float32)
    sigmoid_gate = jax.nn.sigmoid(gate_pre)
    activated = gate_pre * sigmoid_gate
    hidden = (activated * up_pre).astype(jnp.bfloat16)
    out_rows = jnp.einsum(
        "erf,efd->erd", hidden, full_down, preferred_element_type=jnp.float32
    ).astype(jnp.bfloat16)
    d_hidden = jnp.einsum("erd,efd->erf", rows_cot, full_down, preferred_element_type=jnp.float32)
    d_gate = (d_hidden * up_pre * (sigmoid_gate + activated * (1.0 - sigmoid_gate))).astype(
        jnp.bfloat16
    )
    d_up = (d_hidden * activated).astype(jnp.bfloat16)
    dx_rows = jnp.einsum("erf,efd->erd", d_gate, full_gate, preferred_element_type=jnp.float32)
    dx_rows = (
        dx_rows + jnp.einsum("erf,efd->erd", d_up, full_up, preferred_element_type=jnp.float32)
    ).astype(jnp.bfloat16)
    part_down = jnp.einsum("erf,erd->efd", hidden, rows_cot, preferred_element_type=jnp.float32)
    part_gate = jnp.einsum("erf,erd->efd", d_gate, rows_in, preferred_element_type=jnp.float32)
    part_up = jnp.einsum("erf,erd->efd", d_up, rows_in, preferred_element_type=jnp.float32)

    out_rows = out_rows.reshape(local_experts, n_in, 2, slots, width)
    dx_rows = dx_rows.reshape(local_experts, n_in, 2, slots, width)

    def returning(which):
        back = jnp.stack([out_rows[:, :, which], dx_rows[:, :, which]], axis=2)
        back = back.transpose(1, 0, 2, 3, 4).reshape(half_experts, 2, slots, width)
        return lax.all_to_all(back, "inner", split_axis=0, concat_axis=0, tiled=True)

    parts = jnp.concatenate([part_gate, part_up, part_down], axis=0)
    summed = parts[:, :hidden_part]
    for d in range(1, n_dp):
        block = parts[:, d * hidden_part : (d + 1) * hidden_part].astype(jnp.bfloat16)
        summed = summed + shifted(block, "dp", n_dp, -d).astype(jnp.float32)
    summed = summed.astype(jnp.bfloat16)
    grad_gate_w = summed[:local_experts]
    grad_up_w = summed[local_experts : 2 * local_experts]
    grad_down_w = summed[2 * local_experts :]

    place = jnp.where(inside, local * slots + all_code % slots, half_rows)
    columns = jnp.arange(half_rows, dtype=jnp.int32)

    def combine(which):
        back = returning(which)
        out_part = back[:, 0].reshape(half_rows, width)
        dx_part = back[:, 1].reshape(half_rows, width)
        rows = slice(which * tok_rows, (which + 1) * tok_rows)
        hit = place[rows][:, :, None] == columns[None, None, :]
        weight = jnp.sum(jnp.where(hit, all_gates[rows][:, :, None], 0.0), axis=1)
        ones = jnp.sum(hit.astype(jnp.float32), axis=1).astype(jnp.bfloat16)
        layer = jnp.dot(in_three(weight), out_part, preferred_element_type=jnp.float32)
        layer = layer[:tok_rows] + layer[tok_rows : 2 * tok_rows] + layer[2 * tok_rows :]
        grads = jnp.dot(ones, dx_part, preferred_element_type=jnp.float32)
        scores = jnp.dot(all_rows[rows, width:], out_part.T, preferred_element_type=jnp.float32)
        gg = jnp.sum(jnp.where(hit, scores[:, None, :], 0.0), axis=2)
        return layer, grads, gg

    partner_layer, partner_grads, partner_gg = combine(1)
    returned = shifted(
        jnp.concatenate([partner_layer, partner_grads], axis=1).astype(jnp.bfloat16), "half", 2, 1
    )
    returned_gg = shifted(partner_gg, "half", 2, 1)
    own_layer, own_grads, own_gg = combine(0)
    layer_out = (own_layer + returned[:, :width].astype(jnp.float32)).astype(jnp.bfloat16)
    grad_tokens = (own_grads + returned[:, width:].astype(jnp.float32)).astype(jnp.bfloat16)
    grad_gates = own_gg + returned_gg
    return (layer_out, grad_tokens, grad_gates, grad_gate_w, grad_up_w, grad_down_w)


def solution(mesh):
    n_expert = mesh.shape["expert"]
    n_dp = mesh.shape["dp"]
    devices = np.asarray(mesh.devices).reshape(2, n_expert // 2, n_dp)
    split = Mesh(devices, ("half", "inner", "dp"))
    rows = P(("half", "inner", "dp"), None)
    weights = P(("half", "inner"), "dp", None)
    return jax.shard_map(
        on_device,
        mesh=split,
        in_specs=(rows, rows, rows, rows, P(), weights, weights, weights),
        out_specs=(rows, rows, rows, weights, weights, weights),
        check_vma=False,
    )
```

```python
import jax
import jax.numpy as jnp
import numpy as np
from jax import lax
from jax.sharding import Mesh
from jax.sharding import PartitionSpec as P


def shifted(value, axis, count, shift):
    return lax.ppermute(value, axis, [(j, (j + shift) % count) for j in range(count)])


def in_three(value):
    first = value.astype(jnp.bfloat16)
    rest = value - first.astype(jnp.float32)
    second = rest.astype(jnp.bfloat16)
    third = (rest - second.astype(jnp.float32)).astype(jnp.bfloat16)
    return jnp.concatenate([first, second, third], axis=0)


def on_device(tokens, cotangent, expert_ids, gate_vals, capacity, w_gate, w_up, w_down):
    tok_rows, width = tokens.shape
    top_count = expert_ids.shape[1]
    experts = capacity.shape[0]
    local_experts, hidden_part, _ = w_gate.shape
    slots = max(2, (5 * tok_rows * top_count + 4 * experts - 1) // (4 * experts))
    n_in = lax.axis_size("inner")
    n_dp = lax.axis_size("dp")
    half = lax.axis_index("half")
    inner = lax.axis_index("inner")
    source = half * n_in + inner
    n_src = 2 * n_in
    half_experts = n_in * local_experts
    half_rows = half_experts * slots

    weights = jnp.concatenate([w_gate, w_up, w_down], axis=0)
    pieces = [weights] + [shifted(weights, "dp", n_dp, d) for d in range(1, n_dp)]

    both_rows = jnp.concatenate([tokens, cotangent], axis=1)
    partner_rows = shifted(both_rows, "half", 2, 1)
    partner_gates = shifted(gate_vals, "half", 2, 1)

    flat_ids = expert_ids.reshape(-1)
    one_hot = (flat_ids[:, None] == jnp.arange(experts, dtype=jnp.int32)[None, :]).astype(jnp.int32)
    running = jnp.cumsum(one_hot, axis=0)
    local_rank = jnp.sum(running * one_hot, axis=1) - 1
    code = (flat_ids * slots + local_rank).reshape(tok_rows, top_count)
    partner_code = shifted(code, "half", 2, 1)

    all_rows = jnp.concatenate([both_rows, partner_rows], axis=0)
    all_gates = jnp.concatenate([gate_vals, partner_gates], axis=0)
    all_code = jnp.concatenate([code, partner_code], axis=0)
    local = all_code // slots - half * half_experts
    inside = (local >= 0) & (local < half_experts)
    side = (jnp.arange(2 * tok_rows, dtype=jnp.int32) >= tok_rows).astype(jnp.int32)[:, None]
    chunk = 2 * slots + 8
    dest = jnp.where(inside, local * chunk + side * slots + all_code % slots, half_experts * chunk)

    row_of = jnp.broadcast_to(jnp.arange(2 * tok_rows, dtype=jnp.int32)[:, None], dest.shape)
    filled_by = jnp.full((half_experts * chunk,), -1, jnp.int32).at[dest.reshape(-1)].set(
        row_of.reshape(-1), mode="drop"
    )
    slot_gate = jnp.zeros((half_experts * chunk,), jnp.float32).at[dest.reshape(-1)].set(
        all_gates.reshape(-1), mode="drop"
    )
    pick = (filled_by[:, None] == jnp.arange(2 * tok_rows, dtype=jnp.int32)[None, :]).astype(
        jnp.bfloat16
    )
    picked = jnp.dot(pick, all_rows, preferred_element_type=jnp.float32)
    named = (local[None] == jnp.arange(half_experts, dtype=jnp.int32)[:, None, None]) & (
        side[None] == jnp.arange(2, dtype=jnp.int32)[:, None, None, None]
    )
    half_counts = jnp.sum(named.astype(jnp.int32), axis=(2, 3)).T
    place_row = jnp.arange(half_experts * chunk, dtype=jnp.int32)[:, None]
    lane = jnp.arange(2 * width, dtype=jnp.int32)[None, :]
    spare = place_row % chunk == 2 * slots
    owner = place_row // chunk
    count_value = jnp.where(
        lane == 0, half_counts[owner[:, 0], 0][:, None], half_counts[owner[:, 0], 1][:, None]
    ).astype(jnp.float32)
    send_x = picked[:, :width]
    send_c = slot_gate[:, None] * picked[:, width:]
    send = jnp.concatenate([send_x, send_c], axis=1)
    send = jnp.where(spare & (lane < 2), count_value, send).astype(jnp.bfloat16)
    send = send.reshape(half_experts, chunk, 2 * width)
    got = lax.all_to_all(send, "inner", split_axis=0, concat_axis=0, tiled=True)
    got = got.reshape(n_in, local_experts, chunk, 2 * width)

    at_row = (jnp.arange(chunk, dtype=jnp.int32) == 2 * slots)[:, None]
    lane_of = jnp.arange(2 * width, dtype=jnp.int32)[None, :]
    sent = jnp.stack(
        [
            jnp.sum(jnp.where(at_row & (lane_of == k), got, 0).astype(jnp.float32), axis=(2, 3))
            for k in range(2)
        ],
        axis=-1,
    ).astype(jnp.int32)
    by_source = jnp.where(
        half == 0,
        jnp.concatenate([sent[:, :, 0], sent[:, :, 1]], axis=0),
        jnp.concatenate([sent[:, :, 1], sent[:, :, 0]], axis=0),
    )
    earlier = jnp.cumsum(by_source, axis=0) - by_source
    holders = jnp.arange(n_in, dtype=jnp.int32)[:, None]
    halves = jnp.stack([half, 1 - half])[None, :]
    sources = halves * n_in + holders
    mine = (half * n_in + inner) * local_experts + jnp.arange(local_experts, dtype=jnp.int32)
    before = earlier[sources].transpose(0, 2, 1)
    position = jnp.arange(chunk, dtype=jnp.int32)
    ranks = position % slots
    which_side = jnp.minimum(position // slots, 1)
    start = jnp.where(which_side == 0, before[..., 0, None], before[..., 1, None])
    keep = (position < 2 * slots) & (start + ranks < capacity[mine][None, :, None])
    got = jnp.where(keep[..., None], got, jnp.zeros((), got.dtype))
    if local_experts == 1:
        got = got.reshape(1, n_in * chunk, 2 * width)
    else:
        got = got.transpose(1, 0, 2, 3).reshape(local_experts, n_in * chunk, 2 * width)
    rows_in = got[:, :, :width]
    rows_cot = got[:, :, width:]

    full = jnp.concatenate(pieces, axis=1)
    full_gate = full[:local_experts]
    full_up = full[local_experts : 2 * local_experts]
    full_down = full[2 * local_experts :]

    gate_pre = jnp.einsum("erd,efd->erf", rows_in, full_gate, preferred_element_type=jnp.float32)
    up_pre = jnp.einsum("erd,efd->erf", rows_in, full_up, preferred_element_type=jnp.float32)
    sigmoid_gate = jax.nn.sigmoid(gate_pre)
    activated = gate_pre * sigmoid_gate
    hidden = (activated * up_pre).astype(jnp.bfloat16)
    out_rows = jnp.einsum(
        "erf,efd->erd", hidden, full_down, preferred_element_type=jnp.float32
    ).astype(jnp.bfloat16)
    d_hidden = jnp.einsum("erd,efd->erf", rows_cot, full_down, preferred_element_type=jnp.float32)
    d_gate = (d_hidden * up_pre * (sigmoid_gate + activated * (1.0 - sigmoid_gate))).astype(
        jnp.bfloat16
    )
    d_up = (d_hidden * activated).astype(jnp.bfloat16)
    dx_rows = jnp.einsum("erf,efd->erd", d_gate, full_gate, preferred_element_type=jnp.float32)
    dx_rows = (
        dx_rows + jnp.einsum("erf,efd->erd", d_up, full_up, preferred_element_type=jnp.float32)
    ).astype(jnp.bfloat16)
    part_down = jnp.einsum("erf,erd->efd", hidden, rows_cot, preferred_element_type=jnp.float32)
    part_gate = jnp.einsum("erf,erd->efd", d_gate, rows_in, preferred_element_type=jnp.float32)
    part_up = jnp.einsum("erf,erd->efd", d_up, rows_in, preferred_element_type=jnp.float32)

    back = jnp.stack([out_rows, dx_rows], axis=1)
    back = back.reshape(local_experts, 2, n_in, chunk, width).transpose(2, 0, 1, 3, 4)
    back = back.reshape(half_experts, 2, chunk, width)
    back = lax.all_to_all(back, "inner", split_axis=0, concat_axis=0, tiled=True)

    parts = jnp.concatenate([part_gate, part_up, part_down], axis=0)
    summed = parts[:, :hidden_part]
    for d in range(1, n_dp):
        block = parts[:, d * hidden_part : (d + 1) * hidden_part].astype(jnp.bfloat16)
        summed = summed + shifted(block, "dp", n_dp, -d).astype(jnp.float32)
    summed = summed.astype(jnp.bfloat16)
    grad_gate_w = summed[:local_experts]
    grad_up_w = summed[local_experts : 2 * local_experts]
    grad_down_w = summed[2 * local_experts :]

    out_part = back[:, 0].reshape(half_experts * chunk, width)
    dx_part = back[:, 1].reshape(half_experts * chunk, width)
    hit = dest[:, :, None] == jnp.arange(half_experts * chunk, dtype=jnp.int32)[None, None, :]
    weight = jnp.sum(jnp.where(hit, all_gates[:, :, None], 0.0), axis=1)
    ones = jnp.sum(hit.astype(jnp.float32), axis=1).astype(jnp.bfloat16)
    layer = jnp.dot(in_three(weight), out_part, preferred_element_type=jnp.float32)
    n_all = 2 * tok_rows
    layer = layer[:n_all] + layer[n_all : 2 * n_all] + layer[2 * n_all :]
    grads = jnp.dot(ones, dx_part, preferred_element_type=jnp.float32)
    scores = jnp.dot(all_rows[:, width:], out_part.T, preferred_element_type=jnp.float32)
    gg = jnp.sum(jnp.where(hit, scores[:, None, :], 0.0), axis=2)

    returned = shifted(
        jnp.concatenate([layer[tok_rows:], grads[tok_rows:]], axis=1).astype(jnp.bfloat16),
        "half",
        2,
        1,
    )
    returned_gg = shifted(gg[tok_rows:], "half", 2, 1)
    layer_out = (layer[:tok_rows] + returned[:, :width].astype(jnp.float32)).astype(jnp.bfloat16)
    grad_tokens = (grads[:tok_rows] + returned[:, width:].astype(jnp.float32)).astype(jnp.bfloat16)
    grad_gates = gg[:tok_rows] + returned_gg
    return (layer_out, grad_tokens, grad_gates, grad_gate_w, grad_up_w, grad_down_w)


def solution(mesh):
    n_expert = mesh.shape["expert"]
    n_dp = mesh.shape["dp"]
    devices = np.asarray(mesh.devices).reshape(2, n_expert // 2, n_dp)
    split = Mesh(devices, ("half", "inner", "dp"))
    rows = P(("half", "inner", "dp"), None)
    weights = P(("half", "inner"), "dp", None)
    return jax.shard_map(
        on_device,
        mesh=split,
        in_specs=(rows, rows, rows, rows, P(), weights, weights, weights),
        out_specs=(rows, rows, rows, weights, weights, weights),
        check_vma=False,
    )
```

```python
import jax
import jax.numpy as jnp
import numpy as np
from jax import lax
from jax.sharding import Mesh
from jax.sharding import PartitionSpec as P


def shifted(value, axis, count, shift):
    return lax.ppermute(value, axis, [(j, (j + shift) % count) for j in range(count)])


def in_three(value):
    first = value.astype(jnp.bfloat16)
    rest = value - first.astype(jnp.float32)
    second = rest.astype(jnp.bfloat16)
    third = (rest - second.astype(jnp.float32)).astype(jnp.bfloat16)
    return jnp.concatenate([first, second, third], axis=0)


def on_device(tokens, cotangent, expert_ids, gate_vals, capacity, w_gate, w_up, w_down):
    tok_rows, width = tokens.shape
    top_count = expert_ids.shape[1]
    experts = capacity.shape[0]
    local_experts, hidden_part, _ = w_gate.shape
    slots = max(2, (5 * tok_rows * top_count + 4 * experts - 1) // (4 * experts))
    n_in = lax.axis_size("inner")
    n_dp = lax.axis_size("dp")
    half = lax.axis_index("half")
    inner = lax.axis_index("inner")
    source = half * n_in + inner
    n_src = 2 * n_in
    half_experts = n_in * local_experts
    half_rows = half_experts * slots

    weights = jnp.concatenate([w_gate, w_up, w_down], axis=0)
    pieces = [weights] + [shifted(weights, "dp", n_dp, d) for d in range(1, n_dp)]

    both_rows = jnp.concatenate([tokens, cotangent], axis=1)
    partner_rows = shifted(both_rows, "half", 2, 1)
    partner_gates = shifted(gate_vals, "half", 2, 1)

    flat_ids = expert_ids.reshape(-1)
    one_hot = (flat_ids[:, None] == jnp.arange(experts, dtype=jnp.int32)[None, :]).astype(jnp.int32)
    running = jnp.cumsum(one_hot, axis=0)
    local_rank = jnp.sum(running * one_hot, axis=1) - 1
    code = (flat_ids * slots + local_rank).reshape(tok_rows, top_count)
    partner_code = shifted(code, "half", 2, 1)

    all_rows = jnp.concatenate([both_rows, partner_rows], axis=0)
    all_gates = jnp.concatenate([gate_vals, partner_gates], axis=0)
    all_code = jnp.concatenate([code, partner_code], axis=0)
    local = all_code // slots - half * half_experts
    inside = (local >= 0) & (local < half_experts)
    side = (jnp.arange(2 * tok_rows, dtype=jnp.int32) >= tok_rows).astype(jnp.int32)[:, None]
    chunk = 2 * slots + 8
    dest = jnp.where(inside, local * chunk + side * slots + all_code % slots, half_experts * chunk)

    row_of = jnp.broadcast_to(jnp.arange(2 * tok_rows, dtype=jnp.int32)[:, None], dest.shape)
    filled_by = jnp.full((half_experts * chunk,), -1, jnp.int32).at[dest.reshape(-1)].set(
        row_of.reshape(-1), mode="drop"
    )
    slot_gate = jnp.zeros((half_experts * chunk,), jnp.float32).at[dest.reshape(-1)].set(
        all_gates.reshape(-1), mode="drop"
    )
    pick = (filled_by[:, None] == jnp.arange(2 * tok_rows, dtype=jnp.int32)[None, :]).astype(
        jnp.bfloat16
    )
    picked = jnp.dot(pick, all_rows, preferred_element_type=jnp.float32)
    named = (local[None] == jnp.arange(half_experts, dtype=jnp.int32)[:, None, None]) & (
        side[None] == jnp.arange(2, dtype=jnp.int32)[:, None, None, None]
    )
    half_counts = jnp.sum(named.astype(jnp.int32), axis=(2, 3)).T
    lane = jnp.arange(2 * width, dtype=jnp.int32)[None, None, :]
    spare = (jnp.arange(chunk, dtype=jnp.int32) == 2 * slots)[None, :, None] & (lane < 2)
    count_value = jnp.where(
        lane == 0, half_counts[:, 0, None, None], half_counts[:, 1, None, None]
    ).astype(jnp.float32)
    send_x = picked[:, :width]
    send_c = slot_gate[:, None] * picked[:, width:]
    send = jnp.concatenate([send_x, send_c], axis=1).reshape(half_experts, chunk, 2 * width)
    send = jnp.where(spare, count_value, send).astype(jnp.bfloat16)
    got = lax.all_to_all(send, "inner", split_axis=0, concat_axis=0, tiled=True)
    got = got.reshape(n_in, local_experts, chunk, 2 * width)

    at_row = (jnp.arange(chunk, dtype=jnp.int32) == 2 * slots)[:, None]
    lane_of = jnp.arange(2 * width, dtype=jnp.int32)[None, :]
    sent = jnp.stack(
        [
            jnp.sum(jnp.where(at_row & (lane_of == k), got, 0).astype(jnp.float32), axis=(2, 3))
            for k in range(2)
        ],
        axis=-1,
    ).astype(jnp.int32)
    by_source = jnp.where(
        half == 0,
        jnp.concatenate([sent[:, :, 0], sent[:, :, 1]], axis=0),
        jnp.concatenate([sent[:, :, 1], sent[:, :, 0]], axis=0),
    )
    earlier = jnp.cumsum(by_source, axis=0) - by_source
    holders = jnp.arange(n_in, dtype=jnp.int32)[:, None]
    halves = jnp.stack([half, 1 - half])[None, :]
    sources = halves * n_in + holders
    mine = (half * n_in + inner) * local_experts + jnp.arange(local_experts, dtype=jnp.int32)
    before = earlier[sources].transpose(0, 2, 1)
    position = jnp.arange(chunk, dtype=jnp.int32)
    ranks = position % slots
    which_side = jnp.minimum(position // slots, 1)
    start = jnp.where(which_side == 0, before[..., 0, None], before[..., 1, None])
    keep = (position < 2 * slots) & (start + ranks < capacity[mine][None, :, None])
    got = jnp.where(keep[..., None], got, jnp.zeros((), got.dtype))
    if local_experts == 1:
        got = got.reshape(1, n_in * chunk, 2 * width)
    else:
        got = got.transpose(1, 0, 2, 3).reshape(local_experts, n_in * chunk, 2 * width)
    rows_in = got[:, :, :width]
    rows_cot = got[:, :, width:]

    full = jnp.concatenate(pieces, axis=1)
    full_gate = full[:local_experts]
    full_up = full[local_experts : 2 * local_experts]
    full_down = full[2 * local_experts :]

    gate_pre = jnp.einsum("erd,efd->erf", rows_in, full_gate, preferred_element_type=jnp.float32)
    up_pre = jnp.einsum("erd,efd->erf", rows_in, full_up, preferred_element_type=jnp.float32)
    sigmoid_gate = jax.nn.sigmoid(gate_pre)
    activated = gate_pre * sigmoid_gate
    hidden = (activated * up_pre).astype(jnp.bfloat16)
    out_rows = jnp.einsum(
        "erf,efd->erd", hidden, full_down, preferred_element_type=jnp.float32
    ).astype(jnp.bfloat16)
    d_hidden = jnp.einsum("erd,efd->erf", rows_cot, full_down, preferred_element_type=jnp.float32)
    d_gate = (d_hidden * up_pre * (sigmoid_gate + activated * (1.0 - sigmoid_gate))).astype(
        jnp.bfloat16
    )
    d_up = (d_hidden * activated).astype(jnp.bfloat16)
    dx_rows = jnp.einsum("erf,efd->erd", d_gate, full_gate, preferred_element_type=jnp.float32)
    dx_rows = (
        dx_rows + jnp.einsum("erf,efd->erd", d_up, full_up, preferred_element_type=jnp.float32)
    ).astype(jnp.bfloat16)
    part_down = jnp.einsum("erf,erd->efd", hidden, rows_cot, preferred_element_type=jnp.float32)
    part_gate = jnp.einsum("erf,erd->efd", d_gate, rows_in, preferred_element_type=jnp.float32)
    part_up = jnp.einsum("erf,erd->efd", d_up, rows_in, preferred_element_type=jnp.float32)

    back = jnp.stack([out_rows, dx_rows], axis=1)
    back = back.reshape(local_experts, 2, n_in, chunk, width).transpose(2, 0, 1, 3, 4)
    back = back.reshape(half_experts, 2, chunk, width)
    back = lax.all_to_all(back, "inner", split_axis=0, concat_axis=0, tiled=True)

    parts = jnp.concatenate([part_gate, part_up, part_down], axis=0)
    summed = parts[:, :hidden_part]
    for d in range(1, n_dp):
        block = parts[:, d * hidden_part : (d + 1) * hidden_part].astype(jnp.bfloat16)
        summed = summed + shifted(block, "dp", n_dp, -d).astype(jnp.float32)
    summed = summed.astype(jnp.bfloat16)
    grad_gate_w = summed[:local_experts]
    grad_up_w = summed[local_experts : 2 * local_experts]
    grad_down_w = summed[2 * local_experts :]

    out_part = back[:, 0].reshape(half_experts * chunk, width)
    dx_part = back[:, 1].reshape(half_experts * chunk, width)
    hit = dest[:, :, None] == jnp.arange(half_experts * chunk, dtype=jnp.int32)[None, None, :]
    weight = jnp.sum(jnp.where(hit, all_gates[:, :, None], 0.0), axis=1)
    ones = jnp.sum(hit.astype(jnp.float32), axis=1).astype(jnp.bfloat16)
    layer = jnp.dot(in_three(weight), out_part, preferred_element_type=jnp.float32)
    n_all = 2 * tok_rows
    layer = layer[:n_all] + layer[n_all : 2 * n_all] + layer[2 * n_all :]
    grads = jnp.dot(ones, dx_part, preferred_element_type=jnp.float32)
    scores = jnp.dot(all_rows[:, width:], out_part.T, preferred_element_type=jnp.float32)
    gg = jnp.sum(jnp.where(hit, scores[:, None, :], 0.0), axis=2)

    returned = shifted(
        jnp.concatenate([layer[tok_rows:], grads[tok_rows:]], axis=1).astype(jnp.bfloat16),
        "half",
        2,
        1,
    )
    returned_gg = shifted(gg[tok_rows:], "half", 2, 1)
    layer_out = (layer[:tok_rows] + returned[:, :width].astype(jnp.float32)).astype(jnp.bfloat16)
    grad_tokens = (grads[:tok_rows] + returned[:, width:].astype(jnp.float32)).astype(jnp.bfloat16)
    grad_gates = gg[:tok_rows] + returned_gg
    return (layer_out, grad_tokens, grad_gates, grad_gate_w, grad_up_w, grad_down_w)


def solution(mesh):
    n_expert = mesh.shape["expert"]
    n_dp = mesh.shape["dp"]
    devices = np.asarray(mesh.devices).reshape(2, n_expert // 2, n_dp)
    split = Mesh(devices, ("half", "inner", "dp"))
    rows = P(("half", "inner", "dp"), None)
    weights = P(("half", "inner"), "dp", None)
    return jax.shard_map(
        on_device,
        mesh=split,
        in_specs=(rows, rows, rows, rows, P(), weights, weights, weights),
        out_specs=(rows, rows, rows, weights, weights, weights),
        check_vma=False,
    )
```

```python
import jax
import jax.numpy as jnp
import numpy as np
from jax import lax
from jax.sharding import Mesh
from jax.sharding import PartitionSpec as P


def shifted(value, axis, count, shift):
    return lax.ppermute(value, axis, [(j, (j + shift) % count) for j in range(count)])


def in_three(value):
    first = value.astype(jnp.bfloat16)
    rest = value - first.astype(jnp.float32)
    second = rest.astype(jnp.bfloat16)
    third = (rest - second.astype(jnp.float32)).astype(jnp.bfloat16)
    return jnp.concatenate([first, second, third], axis=0)


def on_device(tokens, cotangent, expert_ids, gate_vals, capacity, w_gate, w_up, w_down):
    tok_rows, width = tokens.shape
    top_count = expert_ids.shape[1]
    experts = capacity.shape[0]
    local_experts, hidden_part, _ = w_gate.shape
    slots = max(2, (5 * tok_rows * top_count + 4 * experts - 1) // (4 * experts))
    n_in = lax.axis_size("inner")
    n_dp = lax.axis_size("dp")
    half = lax.axis_index("half")
    inner = lax.axis_index("inner")
    source = half * n_in + inner
    n_src = 2 * n_in
    half_experts = n_in * local_experts
    half_rows = half_experts * slots

    weights = jnp.concatenate([w_gate, w_up, w_down], axis=0)
    pieces = [weights] + [shifted(weights, "dp", n_dp, d) for d in range(1, n_dp)]

    both_rows = jnp.concatenate([tokens, cotangent], axis=1)
    partner_rows = shifted(both_rows, "half", 2, 1)
    partner_gates = shifted(gate_vals, "half", 2, 1)

    flat_ids = expert_ids.reshape(-1)
    one_hot = (flat_ids[:, None] == jnp.arange(experts, dtype=jnp.int32)[None, :]).astype(jnp.int32)
    running = jnp.cumsum(one_hot, axis=0)
    local_rank = jnp.sum(running * one_hot, axis=1) - 1
    counts = running[-1]
    count_rows = jnp.where(jnp.arange(n_src, dtype=jnp.int32)[:, None] == source, counts[None, :], 0)
    all_counts = lax.psum(count_rows, ("half", "inner"))
    code = (flat_ids * slots + local_rank).reshape(tok_rows, top_count)
    partner_code = shifted(code, "half", 2, 1)

    all_rows = jnp.concatenate([both_rows, partner_rows], axis=0)
    all_gates = jnp.concatenate([gate_vals, partner_gates], axis=0)
    all_code = jnp.concatenate([code, partner_code], axis=0)
    local = all_code // slots - half * half_experts
    inside = (local >= 0) & (local < half_experts)
    side = (jnp.arange(2 * tok_rows, dtype=jnp.int32) >= tok_rows).astype(jnp.int32)[:, None]
    dest = jnp.where(inside, (local * 2 + side) * slots + all_code % slots, 2 * half_rows)

    row_of = jnp.broadcast_to(jnp.arange(2 * tok_rows, dtype=jnp.int32)[:, None], dest.shape)
    filled_by = jnp.full((2 * half_rows,), -1, jnp.int32).at[dest.reshape(-1)].set(
        row_of.reshape(-1), mode="drop"
    )
    slot_gate = jnp.zeros((2 * half_rows,), jnp.float32).at[dest.reshape(-1)].set(
        all_gates.reshape(-1), mode="drop"
    )
    pick = (filled_by[:, None] == jnp.arange(2 * tok_rows, dtype=jnp.int32)[None, :]).astype(
        jnp.bfloat16
    )
    picked = jnp.dot(pick, all_rows, preferred_element_type=jnp.float32)
    send_x = picked[:, :width].astype(jnp.bfloat16)
    send_c = (slot_gate[:, None] * picked[:, width:]).astype(jnp.bfloat16)
    send = jnp.concatenate([send_x, send_c], axis=1).reshape(half_experts, 2 * slots, 2 * width)
    got = lax.all_to_all(send, "inner", split_axis=0, concat_axis=0, tiled=True)
    got = got.reshape(n_in, local_experts, 2, slots, 2 * width)

    earlier = jnp.cumsum(all_counts, axis=0) - all_counts
    holders = jnp.arange(n_in, dtype=jnp.int32)[:, None]
    halves = jnp.stack([half, 1 - half])[None, :]
    sources = halves * n_in + holders
    mine = (half * n_in + inner) * local_experts + jnp.arange(local_experts, dtype=jnp.int32)
    before = earlier[sources][:, :, mine].transpose(0, 2, 1)
    ranks = jnp.arange(slots, dtype=jnp.int32)
    keep = before[..., None] + ranks < capacity[mine][None, :, None, None]
    got = jnp.where(keep[..., None], got, jnp.zeros((), got.dtype))
    if local_experts == 1:
        got = got.reshape(1, n_in * 2 * slots, 2 * width)
    else:
        got = got.transpose(1, 0, 2, 3, 4).reshape(local_experts, n_in * 2 * slots, 2 * width)
    rows_in = got[:, :, :width]
    rows_cot = got[:, :, width:]

    full = jnp.concatenate(pieces, axis=1)
    full_gate = full[:local_experts]
    full_up = full[local_experts : 2 * local_experts]
    full_down = full[2 * local_experts :]

    gate_pre = jnp.einsum("erd,efd->erf", rows_in, full_gate, preferred_element_type=jnp.float32)
    up_pre = jnp.einsum("erd,efd->erf", rows_in, full_up, preferred_element_type=jnp.float32)
    sigmoid_gate = jax.nn.sigmoid(gate_pre)
    activated = gate_pre * sigmoid_gate
    hidden = (activated * up_pre).astype(jnp.bfloat16)
    out_rows = jnp.einsum(
        "erf,efd->erd", hidden, full_down, preferred_element_type=jnp.float32
    ).astype(jnp.bfloat16)
    d_hidden = jnp.einsum("erd,efd->erf", rows_cot, full_down, preferred_element_type=jnp.float32)
    d_gate = (d_hidden * up_pre * (sigmoid_gate + activated * (1.0 - sigmoid_gate))).astype(
        jnp.bfloat16
    )
    d_up = (d_hidden * activated).astype(jnp.bfloat16)
    dx_rows = jnp.einsum("erf,efd->erd", d_gate, full_gate, preferred_element_type=jnp.float32)
    dx_rows = (
        dx_rows + jnp.einsum("erf,efd->erd", d_up, full_up, preferred_element_type=jnp.float32)
    ).astype(jnp.bfloat16)
    part_down = jnp.einsum("erf,erd->efd", hidden, rows_cot, preferred_element_type=jnp.float32)
    part_gate = jnp.einsum("erf,erd->efd", d_gate, rows_in, preferred_element_type=jnp.float32)
    part_up = jnp.einsum("erf,erd->efd", d_up, rows_in, preferred_element_type=jnp.float32)

    back = jnp.stack([out_rows, dx_rows], axis=1)
    back = back.reshape(local_experts, 2, n_in, 2 * slots, width).transpose(2, 0, 1, 3, 4)
    back = back.reshape(half_experts, 2, 2 * slots, width)
    back = lax.all_to_all(back, "inner", split_axis=0, concat_axis=0, tiled=True)

    parts = jnp.concatenate([part_gate, part_up, part_down], axis=0)
    summed = parts[:, :hidden_part]
    for d in range(1, n_dp):
        block = parts[:, d * hidden_part : (d + 1) * hidden_part].astype(jnp.bfloat16)
        summed = summed + shifted(block, "dp", n_dp, -d).astype(jnp.float32)
    summed = summed.astype(jnp.bfloat16)
    grad_gate_w = summed[:local_experts]
    grad_up_w = summed[local_experts : 2 * local_experts]
    grad_down_w = summed[2 * local_experts :]

    out_part = back[:, 0].reshape(2 * half_rows, width)
    dx_part = back[:, 1].reshape(2 * half_rows, width)
    hit = dest[:, :, None] == jnp.arange(2 * half_rows, dtype=jnp.int32)[None, None, :]
    weight = jnp.sum(jnp.where(hit, all_gates[:, :, None], 0.0), axis=1)
    ones = jnp.sum(hit.astype(jnp.float32), axis=1).astype(jnp.bfloat16)
    layer = jnp.dot(in_three(weight), out_part, preferred_element_type=jnp.float32)
    n_all = 2 * tok_rows
    layer = layer[:n_all] + layer[n_all : 2 * n_all] + layer[2 * n_all :]
    grads = jnp.dot(ones, dx_part, preferred_element_type=jnp.float32)
    scores = jnp.dot(all_rows[:, width:], out_part.T, preferred_element_type=jnp.float32)
    gg = jnp.sum(jnp.where(hit, scores[:, None, :], 0.0), axis=2)

    returned = shifted(
        jnp.concatenate([layer[tok_rows:], grads[tok_rows:]], axis=1).astype(jnp.bfloat16),
        "half",
        2,
        1,
    )
    returned_gg = shifted(gg[tok_rows:], "half", 2, 1)
    layer_out = (layer[:tok_rows] + returned[:, :width].astype(jnp.float32)).astype(jnp.bfloat16)
    grad_tokens = (grads[:tok_rows] + returned[:, width:].astype(jnp.float32)).astype(jnp.bfloat16)
    grad_gates = gg[:tok_rows] + returned_gg
    return (layer_out, grad_tokens, grad_gates, grad_gate_w, grad_up_w, grad_down_w)


def solution(mesh):
    n_expert = mesh.shape["expert"]
    n_dp = mesh.shape["dp"]
    devices = np.asarray(mesh.devices).reshape(2, n_expert // 2, n_dp)
    split = Mesh(devices, ("half", "inner", "dp"))
    rows = P(("half", "inner", "dp"), None)
    weights = P(("half", "inner"), "dp", None)
    return jax.shard_map(
        on_device,
        mesh=split,
        in_specs=(rows, rows, rows, rows, P(), weights, weights, weights),
        out_specs=(rows, rows, rows, weights, weights, weights),
        check_vma=False,
    )
```

```python
import jax
import jax.numpy as jnp
import numpy as np
from jax import lax
from jax.sharding import Mesh
from jax.sharding import PartitionSpec as P


def shifted(value, axis, count, shift):
    return lax.ppermute(value, axis, [(j, (j + shift) % count) for j in range(count)])


def in_three(value):
    first = value.astype(jnp.bfloat16)
    rest = value - first.astype(jnp.float32)
    second = rest.astype(jnp.bfloat16)
    third = (rest - second.astype(jnp.float32)).astype(jnp.bfloat16)
    return jnp.concatenate([first, second, third], axis=0)


def on_device(tokens, cotangent, expert_ids, gate_vals, capacity, w_gate, w_up, w_down):
    tok_rows, width = tokens.shape
    top_count = expert_ids.shape[1]
    experts = capacity.shape[0]
    local_experts, hidden_part, _ = w_gate.shape
    slots = max(2, (5 * tok_rows * top_count + 4 * experts - 1) // (4 * experts))
    n_in = lax.axis_size("inner")
    n_dp = lax.axis_size("dp")
    half = lax.axis_index("half")
    inner = lax.axis_index("inner")
    source = half * n_in + inner
    n_src = 2 * n_in
    half_experts = n_in * local_experts
    half_rows = half_experts * slots

    weights = jnp.concatenate([w_gate, w_up, w_down], axis=0)
    pieces = [weights] + [shifted(weights, "dp", n_dp, d) for d in range(1, n_dp)]

    both_rows = jnp.concatenate([tokens, cotangent], axis=1)
    partner_rows = shifted(both_rows, "half", 2, 1)
    partner_gates = shifted(gate_vals, "half", 2, 1)

    flat_ids = expert_ids.reshape(-1)
    one_hot = (flat_ids[:, None] == jnp.arange(experts, dtype=jnp.int32)[None, :]).astype(jnp.int32)
    running = jnp.cumsum(one_hot, axis=0)
    local_rank = jnp.sum(running * one_hot, axis=1) - 1
    counts = running[-1]
    count_rows = jnp.where(jnp.arange(n_src, dtype=jnp.int32)[:, None] == source, counts[None, :], 0)
    all_counts = lax.psum(count_rows, ("half", "inner"))
    code = (flat_ids * slots + local_rank).reshape(tok_rows, top_count)
    partner_code = shifted(code, "half", 2, 1)

    all_rows = jnp.concatenate([both_rows, partner_rows], axis=0)
    all_gates = jnp.concatenate([gate_vals, partner_gates], axis=0)
    all_code = jnp.concatenate([code, partner_code], axis=0)
    local = all_code // slots - half * half_experts
    inside = (local >= 0) & (local < half_experts)
    side = (jnp.arange(2 * tok_rows, dtype=jnp.int32) >= tok_rows).astype(jnp.int32)[:, None]
    dest = jnp.where(inside, (local * 2 + side) * slots + all_code % slots, 2 * half_rows)

    slot_ids = jnp.arange(2 * half_rows, dtype=jnp.int32)[:, None, None]
    lands = dest[None, :, :] == slot_ids
    pick = jnp.any(lands, axis=2).astype(jnp.bfloat16)
    slot_gate = jnp.sum(jnp.where(lands, all_gates[None, :, :], 0.0), axis=(1, 2))
    picked = jnp.dot(pick, all_rows, preferred_element_type=jnp.float32)
    lane = jnp.arange(2 * width, dtype=jnp.int32)[None, :]
    scale = jnp.where(lane < width, 1.0, slot_gate[:, None])
    send = (picked * scale).astype(jnp.bfloat16).reshape(half_experts, 2 * slots, 2 * width)
    got = lax.all_to_all(send, "inner", split_axis=0, concat_axis=0, tiled=True)
    got = got.reshape(n_in, local_experts, 2, slots, 2 * width)

    earlier = jnp.cumsum(all_counts, axis=0) - all_counts
    holders = jnp.arange(n_in, dtype=jnp.int32)[:, None]
    halves = jnp.stack([half, 1 - half])[None, :]
    sources = halves * n_in + holders
    mine = (half * n_in + inner) * local_experts + jnp.arange(local_experts, dtype=jnp.int32)
    before = earlier[sources][:, :, mine].transpose(0, 2, 1)
    ranks = jnp.arange(slots, dtype=jnp.int32)
    keep = before[..., None] + ranks < capacity[mine][None, :, None, None]
    got = jnp.where(keep[..., None], got, jnp.zeros((), got.dtype))
    if local_experts == 1:
        got = got.reshape(1, n_in * 2 * slots, 2 * width)
    else:
        got = got.transpose(1, 0, 2, 3, 4).reshape(local_experts, n_in * 2 * slots, 2 * width)
    rows_in = got[:, :, :width]
    rows_cot = got[:, :, width:]

    full = jnp.concatenate(pieces, axis=1)
    full_gate = full[:local_experts]
    full_up = full[local_experts : 2 * local_experts]
    full_down = full[2 * local_experts :]

    gate_pre = jnp.einsum("erd,efd->erf", rows_in, full_gate, preferred_element_type=jnp.float32)
    up_pre = jnp.einsum("erd,efd->erf", rows_in, full_up, preferred_element_type=jnp.float32)
    sigmoid_gate = jax.nn.sigmoid(gate_pre)
    activated = gate_pre * sigmoid_gate
    hidden = (activated * up_pre).astype(jnp.bfloat16)
    out_rows = jnp.einsum(
        "erf,efd->erd", hidden, full_down, preferred_element_type=jnp.float32
    ).astype(jnp.bfloat16)
    d_hidden = jnp.einsum("erd,efd->erf", rows_cot, full_down, preferred_element_type=jnp.float32)
    d_gate = (d_hidden * up_pre * (sigmoid_gate + activated * (1.0 - sigmoid_gate))).astype(
        jnp.bfloat16
    )
    d_up = (d_hidden * activated).astype(jnp.bfloat16)
    dx_rows = jnp.einsum("erf,efd->erd", d_gate, full_gate, preferred_element_type=jnp.float32)
    dx_rows = (
        dx_rows + jnp.einsum("erf,efd->erd", d_up, full_up, preferred_element_type=jnp.float32)
    ).astype(jnp.bfloat16)
    part_down = jnp.einsum("erf,erd->efd", hidden, rows_cot, preferred_element_type=jnp.float32)
    part_gate = jnp.einsum("erf,erd->efd", d_gate, rows_in, preferred_element_type=jnp.float32)
    part_up = jnp.einsum("erf,erd->efd", d_up, rows_in, preferred_element_type=jnp.float32)

    back = jnp.stack([out_rows, dx_rows], axis=1)
    back = back.reshape(local_experts, 2, n_in, 2 * slots, width).transpose(2, 0, 1, 3, 4)
    back = back.reshape(half_experts, 2, 2 * slots, width)
    back = lax.all_to_all(back, "inner", split_axis=0, concat_axis=0, tiled=True)

    parts = jnp.concatenate([part_gate, part_up, part_down], axis=0)
    summed = parts[:, :hidden_part]
    for d in range(1, n_dp):
        block = parts[:, d * hidden_part : (d + 1) * hidden_part].astype(jnp.bfloat16)
        summed = summed + shifted(block, "dp", n_dp, -d).astype(jnp.float32)
    summed = summed.astype(jnp.bfloat16)
    grad_gate_w = summed[:local_experts]
    grad_up_w = summed[local_experts : 2 * local_experts]
    grad_down_w = summed[2 * local_experts :]

    out_part = back[:, 0].reshape(2 * half_rows, width)
    dx_part = back[:, 1].reshape(2 * half_rows, width)
    hit = dest[:, :, None] == jnp.arange(2 * half_rows, dtype=jnp.int32)[None, None, :]
    weight = jnp.sum(jnp.where(hit, all_gates[:, :, None], 0.0), axis=1)
    ones = jnp.sum(hit.astype(jnp.float32), axis=1).astype(jnp.bfloat16)
    layer = jnp.dot(in_three(weight), out_part, preferred_element_type=jnp.float32)
    n_all = 2 * tok_rows
    layer = layer[:n_all] + layer[n_all : 2 * n_all] + layer[2 * n_all :]
    grads = jnp.dot(ones, dx_part, preferred_element_type=jnp.float32)
    scores = jnp.dot(all_rows[:, width:], out_part.T, preferred_element_type=jnp.float32)
    gg = jnp.sum(jnp.where(hit, scores[:, None, :], 0.0), axis=2)

    returned = shifted(
        jnp.concatenate([layer[tok_rows:], grads[tok_rows:]], axis=1).astype(jnp.bfloat16),
        "half",
        2,
        1,
    )
    returned_gg = shifted(gg[tok_rows:], "half", 2, 1)
    layer_out = (layer[:tok_rows] + returned[:, :width].astype(jnp.float32)).astype(jnp.bfloat16)
    grad_tokens = (grads[:tok_rows] + returned[:, width:].astype(jnp.float32)).astype(jnp.bfloat16)
    grad_gates = gg[:tok_rows] + returned_gg
    return (layer_out, grad_tokens, grad_gates, grad_gate_w, grad_up_w, grad_down_w)


def solution(mesh):
    n_expert = mesh.shape["expert"]
    n_dp = mesh.shape["dp"]
    devices = np.asarray(mesh.devices).reshape(2, n_expert // 2, n_dp)
    split = Mesh(devices, ("half", "inner", "dp"))
    rows = P(("half", "inner", "dp"), None)
    weights = P(("half", "inner"), "dp", None)
    return jax.shard_map(
        on_device,
        mesh=split,
        in_specs=(rows, rows, rows, rows, P(), weights, weights, weights),
        out_specs=(rows, rows, rows, weights, weights, weights),
        check_vma=False,
    )
```

```python
import jax
import jax.numpy as jnp
import numpy as np
from jax import lax
from jax.sharding import Mesh
from jax.sharding import PartitionSpec as P


def shifted(value, axis, count, shift):
    return lax.ppermute(value, axis, [(j, (j + shift) % count) for j in range(count)])


def in_three(value):
    first = value.astype(jnp.bfloat16)
    rest = value - first.astype(jnp.float32)
    second = rest.astype(jnp.bfloat16)
    third = (rest - second.astype(jnp.float32)).astype(jnp.bfloat16)
    return jnp.concatenate([first, second, third], axis=0)


def on_device(tokens, cotangent, expert_ids, gate_vals, capacity, w_gate, w_up, w_down):
    tok_rows, width = tokens.shape
    top_count = expert_ids.shape[1]
    experts = capacity.shape[0]
    local_experts, hidden_part, _ = w_gate.shape
    slots = max(2, (5 * tok_rows * top_count + 4 * experts - 1) // (4 * experts))
    n_in = lax.axis_size("inner")
    n_dp = lax.axis_size("dp")
    half = lax.axis_index("half")
    inner = lax.axis_index("inner")
    source = half * n_in + inner
    n_src = 2 * n_in
    half_experts = n_in * local_experts
    half_rows = half_experts * slots

    weights = jnp.concatenate([w_gate, w_up, w_down], axis=0)
    pieces = [weights] + [shifted(weights, "dp", n_dp, d) for d in range(1, n_dp)]

    both_rows = jnp.concatenate([tokens, cotangent], axis=1)
    partner_rows = shifted(both_rows, "half", 2, 1)
    partner_gates = shifted(gate_vals, "half", 2, 1)

    flat_ids = expert_ids.reshape(-1)
    one_hot = (flat_ids[:, None] == jnp.arange(experts, dtype=jnp.int32)[None, :]).astype(jnp.int32)
    running = jnp.cumsum(one_hot, axis=0)
    local_rank = jnp.sum(running * one_hot, axis=1) - 1
    counts = running[-1]
    all_counts = lax.all_gather(counts, ("half", "inner"))
    code = (flat_ids * slots + local_rank).reshape(tok_rows, top_count)
    partner_code = shifted(code, "half", 2, 1)

    all_rows = jnp.concatenate([both_rows, partner_rows], axis=0)
    all_gates = jnp.concatenate([gate_vals, partner_gates], axis=0)
    all_code = jnp.concatenate([code, partner_code], axis=0)
    local = all_code // slots - half * half_experts
    inside = (local >= 0) & (local < half_experts)
    side = (jnp.arange(2 * tok_rows, dtype=jnp.int32) >= tok_rows).astype(jnp.int32)[:, None]
    dest = jnp.where(inside, (local * 2 + side) * slots + all_code % slots, 2 * half_rows)

    slot_ids = jnp.arange(2 * half_rows, dtype=jnp.int32)[:, None, None]
    lands = dest[None, :, :] == slot_ids
    pick = jnp.any(lands, axis=2).astype(jnp.bfloat16)
    slot_gate = jnp.sum(jnp.where(lands, all_gates[None, :, :], 0.0), axis=(1, 2))
    picked = jnp.dot(pick, all_rows, preferred_element_type=jnp.float32)
    lane = jnp.arange(2 * width, dtype=jnp.int32)[None, :]
    scale = jnp.where(lane < width, 1.0, slot_gate[:, None])
    send = (picked * scale).astype(jnp.bfloat16).reshape(half_experts, 2 * slots, 2 * width)
    send = jnp.where(all_counts[0, 0] >= 0, send, jnp.zeros((), send.dtype))
    got = lax.all_to_all(send, "inner", split_axis=0, concat_axis=0, tiled=True)
    got = got.reshape(n_in, local_experts, 2, slots, 2 * width)

    earlier = jnp.cumsum(all_counts, axis=0) - all_counts
    holders = jnp.arange(n_in, dtype=jnp.int32)[:, None]
    halves = jnp.stack([half, 1 - half])[None, :]
    sources = halves * n_in + holders
    mine = (half * n_in + inner) * local_experts + jnp.arange(local_experts, dtype=jnp.int32)
    before = earlier[sources][:, :, mine].transpose(0, 2, 1)
    ranks = jnp.arange(slots, dtype=jnp.int32)
    keep = before[..., None] + ranks < capacity[mine][None, :, None, None]
    got = jnp.where(keep[..., None], got, jnp.zeros((), got.dtype))
    if local_experts == 1:
        got = got.reshape(1, n_in * 2 * slots, 2 * width)
    else:
        got = got.transpose(1, 0, 2, 3, 4).reshape(local_experts, n_in * 2 * slots, 2 * width)
    rows_in = got[:, :, :width]
    rows_cot = got[:, :, width:]

    full = jnp.concatenate(pieces, axis=1)
    full_gate = full[:local_experts]
    full_up = full[local_experts : 2 * local_experts]
    full_down = full[2 * local_experts :]

    gate_pre = jnp.einsum("erd,efd->erf", rows_in, full_gate, preferred_element_type=jnp.float32)
    up_pre = jnp.einsum("erd,efd->erf", rows_in, full_up, preferred_element_type=jnp.float32)
    sigmoid_gate = jax.nn.sigmoid(gate_pre)
    activated = gate_pre * sigmoid_gate
    hidden = (activated * up_pre).astype(jnp.bfloat16)
    out_rows = jnp.einsum(
        "erf,efd->erd", hidden, full_down, preferred_element_type=jnp.float32
    ).astype(jnp.bfloat16)
    d_hidden = jnp.einsum("erd,efd->erf", rows_cot, full_down, preferred_element_type=jnp.float32)
    d_gate = (d_hidden * up_pre * (sigmoid_gate + activated * (1.0 - sigmoid_gate))).astype(
        jnp.bfloat16
    )
    d_up = (d_hidden * activated).astype(jnp.bfloat16)
    dx_rows = jnp.einsum("erf,efd->erd", d_gate, full_gate, preferred_element_type=jnp.float32)
    dx_rows = (
        dx_rows + jnp.einsum("erf,efd->erd", d_up, full_up, preferred_element_type=jnp.float32)
    ).astype(jnp.bfloat16)
    part_down = jnp.einsum("erf,erd->efd", hidden, rows_cot, preferred_element_type=jnp.float32)
    part_gate = jnp.einsum("erf,erd->efd", d_gate, rows_in, preferred_element_type=jnp.float32)
    part_up = jnp.einsum("erf,erd->efd", d_up, rows_in, preferred_element_type=jnp.float32)

    back = jnp.stack([out_rows, dx_rows], axis=1)
    back = back.reshape(local_experts, 2, n_in, 2 * slots, width).transpose(2, 0, 1, 3, 4)
    back = back.reshape(half_experts, 2, 2 * slots, width)
    back = lax.all_to_all(back, "inner", split_axis=0, concat_axis=0, tiled=True)

    parts = jnp.concatenate([part_gate, part_up, part_down], axis=0)
    summed = parts[:, :hidden_part]
    for d in range(1, n_dp):
        block = parts[:, d * hidden_part : (d + 1) * hidden_part].astype(jnp.bfloat16)
        summed = summed + shifted(block, "dp", n_dp, -d).astype(jnp.float32)
    summed = summed.astype(jnp.bfloat16)
    grad_gate_w = summed[:local_experts]
    grad_up_w = summed[local_experts : 2 * local_experts]
    grad_down_w = summed[2 * local_experts :]

    out_part = back[:, 0].reshape(2 * half_rows, width)
    dx_part = back[:, 1].reshape(2 * half_rows, width)
    hit = dest[:, :, None] == jnp.arange(2 * half_rows, dtype=jnp.int32)[None, None, :]
    weight = jnp.sum(jnp.where(hit, all_gates[:, :, None], 0.0), axis=1)
    ones = jnp.sum(hit.astype(jnp.float32), axis=1).astype(jnp.bfloat16)
    layer = jnp.dot(in_three(weight), out_part, preferred_element_type=jnp.float32)
    n_all = 2 * tok_rows
    layer = layer[:n_all] + layer[n_all : 2 * n_all] + layer[2 * n_all :]
    grads = jnp.dot(ones, dx_part, preferred_element_type=jnp.float32)
    scores = jnp.dot(all_rows[:, width:], out_part.T, preferred_element_type=jnp.float32)
    gg = jnp.sum(jnp.where(hit, scores[:, None, :], 0.0), axis=2)

    returned = shifted(
        jnp.concatenate([layer[tok_rows:], grads[tok_rows:]], axis=1).astype(jnp.bfloat16),
        "half",
        2,
        1,
    )
    returned_gg = shifted(gg[tok_rows:], "half", 2, 1)
    layer_out = (layer[:tok_rows] + returned[:, :width].astype(jnp.float32)).astype(jnp.bfloat16)
    grad_tokens = (grads[:tok_rows] + returned[:, width:].astype(jnp.float32)).astype(jnp.bfloat16)
    grad_gates = gg[:tok_rows] + returned_gg
    return (layer_out, grad_tokens, grad_gates, grad_gate_w, grad_up_w, grad_down_w)


def solution(mesh):
    n_expert = mesh.shape["expert"]
    n_dp = mesh.shape["dp"]
    devices = np.asarray(mesh.devices).reshape(2, n_expert // 2, n_dp)
    split = Mesh(devices, ("half", "inner", "dp"))
    rows = P(("half", "inner", "dp"), None)
    weights = P(("half", "inner"), "dp", None)
    return jax.shard_map(
        on_device,
        mesh=split,
        in_specs=(rows, rows, rows, rows, P(), weights, weights, weights),
        out_specs=(rows, rows, rows, weights, weights, weights),
        check_vma=False,
    )
```

```python
import jax
import jax.numpy as jnp
import numpy as np
from jax import lax
from jax.sharding import Mesh
from jax.sharding import PartitionSpec as P


def shifted(value, axis, count, shift):
    return lax.ppermute(value, axis, [(j, (j + shift) % count) for j in range(count)])


def in_three(value):
    first = value.astype(jnp.bfloat16)
    rest = value - first.astype(jnp.float32)
    second = rest.astype(jnp.bfloat16)
    third = (rest - second.astype(jnp.float32)).astype(jnp.bfloat16)
    return jnp.concatenate([first, second, third], axis=0)


def on_device(tokens, cotangent, expert_ids, gate_vals, capacity, w_gate, w_up, w_down):
    tok_rows, width = tokens.shape
    top_count = expert_ids.shape[1]
    experts = capacity.shape[0]
    local_experts, hidden_part, _ = w_gate.shape
    slots = max(2, (5 * tok_rows * top_count + 4 * experts - 1) // (4 * experts))
    n_in = lax.axis_size("inner")
    n_dp = lax.axis_size("dp")
    half = lax.axis_index("half")
    inner = lax.axis_index("inner")
    source = half * n_in + inner
    n_src = 2 * n_in
    half_experts = n_in * local_experts
    half_rows = half_experts * slots

    weights = jnp.concatenate([w_gate, w_up, w_down], axis=0)
    pieces = [weights] + [shifted(weights, "dp", n_dp, d) for d in range(1, n_dp)]

    both_rows = jnp.concatenate([tokens, cotangent], axis=1)
    partner_rows = shifted(both_rows, "half", 2, 1)
    partner_gates = shifted(gate_vals, "half", 2, 1)

    flat_ids = expert_ids.reshape(-1)
    one_hot = (flat_ids[:, None] == jnp.arange(experts, dtype=jnp.int32)[None, :]).astype(jnp.int32)
    running = jnp.cumsum(one_hot, axis=0)
    local_rank = jnp.sum(running * one_hot, axis=1) - 1
    counts = running[-1]
    count_rows = jnp.where(jnp.arange(n_src, dtype=jnp.int32)[:, None] == source, counts[None, :], 0)
    all_counts = lax.psum(count_rows, ("half", "inner"))
    code = (flat_ids * slots + local_rank).reshape(tok_rows, top_count)
    partner_code = shifted(code, "half", 2, 1)

    all_rows = jnp.concatenate([both_rows, partner_rows], axis=0)
    all_gates = jnp.concatenate([gate_vals, partner_gates], axis=0)
    all_code = jnp.concatenate([code, partner_code], axis=0)
    local = all_code // slots - half * half_experts
    inside = (local >= 0) & (local < half_experts)
    side = (jnp.arange(2 * tok_rows, dtype=jnp.int32) >= tok_rows).astype(jnp.int32)[:, None]
    dest = jnp.where(inside, (local * 2 + side) * slots + all_code % slots, 2 * half_rows)

    slot_ids = jnp.arange(2 * half_rows, dtype=jnp.int32)[:, None, None]
    lands = dest[None, :, :] == slot_ids
    pick = jnp.any(lands, axis=2).astype(jnp.bfloat16)
    slot_gate = jnp.sum(jnp.where(lands, all_gates[None, :, :], 0.0), axis=(1, 2))
    picked = jnp.dot(pick, all_rows, preferred_element_type=jnp.float32)
    lane = jnp.arange(2 * width, dtype=jnp.int32)[None, :]
    scale = jnp.where(lane < width, 1.0, slot_gate[:, None])
    send = (picked * scale).astype(jnp.bfloat16).reshape(half_experts, 2 * slots, 2 * width)
    got = lax.all_to_all(send, "inner", split_axis=0, concat_axis=0, tiled=True)
    got = got.reshape(n_in, local_experts, 2, slots, 2 * width)

    earlier = jnp.cumsum(all_counts, axis=0) - all_counts
    holders = jnp.arange(n_in, dtype=jnp.int32)[:, None]
    halves = jnp.stack([half, 1 - half])[None, :]
    sources = halves * n_in + holders
    mine = (half * n_in + inner) * local_experts + jnp.arange(local_experts, dtype=jnp.int32)
    before = earlier[sources][:, :, mine].transpose(0, 2, 1)
    ranks = jnp.arange(slots, dtype=jnp.int32)
    keep = before[..., None] + ranks < capacity[mine][None, :, None, None]
    got = jnp.where(keep[..., None], got, jnp.zeros((), got.dtype))
    if local_experts == 1:
        got = got.reshape(1, n_in * 2 * slots, 2 * width)
    else:
        got = got.transpose(1, 0, 2, 3, 4).reshape(local_experts, n_in * 2 * slots, 2 * width)
    rows_in = got[:, :, :width]
    rows_cot = got[:, :, width:]

    full = jnp.concatenate(pieces, axis=1)
    full_gate = full[:local_experts]
    full_up = full[local_experts : 2 * local_experts]
    full_down = full[2 * local_experts :]

    gate_pre = jnp.einsum("erd,efd->erf", rows_in, full_gate, preferred_element_type=jnp.float32)
    up_pre = jnp.einsum("erd,efd->erf", rows_in, full_up, preferred_element_type=jnp.float32)
    sigmoid_gate = jax.nn.sigmoid(gate_pre)
    activated = gate_pre * sigmoid_gate
    hidden = (activated * up_pre).astype(jnp.bfloat16)
    out_rows = jnp.einsum(
        "erf,efd->erd", hidden, full_down, preferred_element_type=jnp.float32
    ).astype(jnp.bfloat16)
    d_hidden = jnp.einsum("erd,efd->erf", rows_cot, full_down, preferred_element_type=jnp.float32)
    d_gate = (d_hidden * up_pre * (sigmoid_gate + activated * (1.0 - sigmoid_gate))).astype(
        jnp.bfloat16
    )
    d_up = (d_hidden * activated).astype(jnp.bfloat16)
    dx_rows = jnp.einsum("erf,efd->erd", d_gate, full_gate, preferred_element_type=jnp.float32)
    dx_rows = (
        dx_rows + jnp.einsum("erf,efd->erd", d_up, full_up, preferred_element_type=jnp.float32)
    ).astype(jnp.bfloat16)
    part_down = jnp.einsum("erf,erd->efd", hidden, rows_cot, preferred_element_type=jnp.float32)
    part_gate = jnp.einsum("erf,erd->efd", d_gate, rows_in, preferred_element_type=jnp.float32)
    part_up = jnp.einsum("erf,erd->efd", d_up, rows_in, preferred_element_type=jnp.float32)

    back = jnp.concatenate([out_rows, dx_rows], axis=-1)
    if local_experts == 1:
        back = back.reshape(half_experts, 2 * slots, 2 * width)
    else:
        back = back.reshape(local_experts, n_in, 2 * slots, 2 * width).transpose(1, 0, 2, 3)
        back = back.reshape(half_experts, 2 * slots, 2 * width)
    back = lax.all_to_all(back, "inner", split_axis=0, concat_axis=0, tiled=True)

    parts = jnp.concatenate([part_gate, part_up, part_down], axis=0)
    summed = parts[:, :hidden_part]
    for d in range(1, n_dp):
        block = parts[:, d * hidden_part : (d + 1) * hidden_part].astype(jnp.bfloat16)
        summed = summed + shifted(block, "dp", n_dp, -d).astype(jnp.float32)
    summed = summed.astype(jnp.bfloat16)
    grad_gate_w = summed[:local_experts]
    grad_up_w = summed[local_experts : 2 * local_experts]
    grad_down_w = summed[2 * local_experts :]

    back = back.reshape(2 * half_rows, 2 * width)
    out_part = back[:, :width]
    dx_part = back[:, width:]
    columns = jnp.arange(2 * half_rows, dtype=jnp.int32)

    def combine(which):
        rows = slice(which * tok_rows, (which + 1) * tok_rows)
        hit = dest[rows][:, :, None] == columns[None, None, :]
        weight = jnp.sum(jnp.where(hit, all_gates[rows][:, :, None], 0.0), axis=1)
        ones = jnp.sum(hit.astype(jnp.float32), axis=1).astype(jnp.bfloat16)
        layer = jnp.dot(in_three(weight), out_part, preferred_element_type=jnp.float32)
        layer = layer[:tok_rows] + layer[tok_rows : 2 * tok_rows] + layer[2 * tok_rows :]
        grads = jnp.dot(ones, dx_part, preferred_element_type=jnp.float32)
        scores = jnp.dot(all_rows[rows, width:], out_part.T, preferred_element_type=jnp.float32)
        gg = jnp.sum(jnp.where(hit, scores[:, None, :], 0.0), axis=2)
        return layer, grads, gg

    partner_layer, partner_grads, partner_gg = combine(1)
    returned = shifted(
        jnp.concatenate([partner_layer, partner_grads], axis=1).astype(jnp.bfloat16), "half", 2, 1
    )
    returned_gg = shifted(partner_gg, "half", 2, 1)
    own_layer, own_grads, own_gg = combine(0)
    layer_out = (own_layer + returned[:, :width].astype(jnp.float32)).astype(jnp.bfloat16)
    grad_tokens = (own_grads + returned[:, width:].astype(jnp.float32)).astype(jnp.bfloat16)
    grad_gates = own_gg + returned_gg
    return (layer_out, grad_tokens, grad_gates, grad_gate_w, grad_up_w, grad_down_w)


def solution(mesh):
    n_expert = mesh.shape["expert"]
    n_dp = mesh.shape["dp"]
    devices = np.asarray(mesh.devices).reshape(2, n_expert // 2, n_dp)
    split = Mesh(devices, ("half", "inner", "dp"))
    rows = P(("half", "inner", "dp"), None)
    weights = P(("half", "inner"), "dp", None)
    return jax.shard_map(
        on_device,
        mesh=split,
        in_specs=(rows, rows, rows, rows, P(), weights, weights, weights),
        out_specs=(rows, rows, rows, weights, weights, weights),
        check_vma=False,
    )
```

```python
import jax
import jax.numpy as jnp
import numpy as np
from jax import lax
from jax.sharding import Mesh
from jax.sharding import PartitionSpec as P


def shifted(value, axis, count, shift):
    return lax.ppermute(value, axis, [(j, (j + shift) % count) for j in range(count)])


def in_three(value):
    first = value.astype(jnp.bfloat16)
    rest = value - first.astype(jnp.float32)
    second = rest.astype(jnp.bfloat16)
    third = (rest - second.astype(jnp.float32)).astype(jnp.bfloat16)
    return jnp.concatenate([first, second, third], axis=0)


def on_device(tokens, cotangent, expert_ids, gate_vals, capacity, w_gate, w_up, w_down):
    tok_rows, width = tokens.shape
    top_count = expert_ids.shape[1]
    experts = capacity.shape[0]
    local_experts, hidden_part, _ = w_gate.shape
    slots = max(2, (5 * tok_rows * top_count + 4 * experts - 1) // (4 * experts))
    n_in = lax.axis_size("inner")
    n_dp = lax.axis_size("dp")
    half = lax.axis_index("half")
    inner = lax.axis_index("inner")
    source = half * n_in + inner
    n_src = 2 * n_in
    half_experts = n_in * local_experts
    half_rows = half_experts * slots

    weights = jnp.concatenate([w_gate, w_up, w_down], axis=0)
    pieces = [weights] + [shifted(weights, "dp", n_dp, d) for d in range(1, n_dp)]

    both_rows = jnp.concatenate([tokens, cotangent], axis=1)
    partner_rows = shifted(both_rows, "half", 2, 1)
    partner_gates = shifted(gate_vals, "half", 2, 1)

    flat_ids = expert_ids.reshape(-1)
    one_hot = (flat_ids[:, None] == jnp.arange(experts, dtype=jnp.int32)[None, :]).astype(jnp.int32)
    running = jnp.cumsum(one_hot, axis=0)
    local_rank = jnp.sum(running * one_hot, axis=1) - 1
    counts = running[-1]
    count_rows = jnp.where(jnp.arange(n_src, dtype=jnp.int32)[:, None] == source, counts[None, :], 0)
    all_counts = lax.psum(count_rows, ("half", "inner"))
    code = (flat_ids * slots + local_rank).reshape(tok_rows, top_count)
    partner_code = shifted(code, "half", 2, 1)

    all_rows = jnp.concatenate([both_rows, partner_rows], axis=0)
    all_gates = jnp.concatenate([gate_vals, partner_gates], axis=0)
    all_code = jnp.concatenate([code, partner_code], axis=0)
    local = all_code // slots - half * half_experts
    inside = (local >= 0) & (local < half_experts)
    side = (jnp.arange(2 * tok_rows, dtype=jnp.int32) >= tok_rows).astype(jnp.int32)[:, None]
    dest = jnp.where(inside, (local * 2 + side) * slots + all_code % slots, 2 * half_rows)

    slot_ids = jnp.arange(2 * half_rows, dtype=jnp.int32)[:, None, None]
    lands = dest[None, :, :] == slot_ids
    pick = jnp.any(lands, axis=2).astype(jnp.bfloat16)
    slot_gate = jnp.sum(jnp.where(lands, all_gates[None, :, :], 0.0), axis=(1, 2))
    picked = jnp.dot(pick, all_rows, preferred_element_type=jnp.float32)
    lane = jnp.arange(2 * width, dtype=jnp.int32)[None, :]
    scale = jnp.where(lane < width, 1.0, slot_gate[:, None])
    send = (picked * scale).astype(jnp.bfloat16).reshape(half_experts, 2 * slots, 2 * width)
    got = lax.all_to_all(send, "inner", split_axis=0, concat_axis=0, tiled=True)
    got = got.reshape(n_in, local_experts, 2, slots, 2 * width)

    earlier = jnp.cumsum(all_counts, axis=0) - all_counts
    holders = jnp.arange(n_in, dtype=jnp.int32)[:, None]
    halves = jnp.stack([half, 1 - half])[None, :]
    sources = halves * n_in + holders
    mine = (half * n_in + inner) * local_experts + jnp.arange(local_experts, dtype=jnp.int32)
    before = earlier[sources][:, :, mine].transpose(0, 2, 1)
    ranks = jnp.arange(slots, dtype=jnp.int32)
    keep = before[..., None] + ranks < capacity[mine][None, :, None, None]
    got = jnp.where(keep[..., None], got, jnp.zeros((), got.dtype))
    if local_experts == 1:
        got = got.reshape(1, n_in * 2 * slots, 2 * width)
    else:
        got = got.transpose(1, 0, 2, 3, 4).reshape(local_experts, n_in * 2 * slots, 2 * width)
    rows_in = got[:, :, :width]
    rows_cot = got[:, :, width:]

    full = jnp.concatenate(pieces, axis=1)
    full_down = full[2 * local_experts :]

    full_hidden = full.shape[1]
    if local_experts == 1:
        gate_up = full[:2].reshape(1, 2 * full_hidden, width)
    else:
        gate_up = full[: 2 * local_experts].reshape(2, local_experts, full_hidden, width)
        gate_up = gate_up.transpose(1, 0, 2, 3).reshape(local_experts, 2 * full_hidden, width)
    both_pre = jnp.einsum("erd,egd->erg", rows_in, gate_up, preferred_element_type=jnp.float32)
    gate_pre = both_pre[..., :full_hidden]
    up_pre = both_pre[..., full_hidden:]
    sigmoid_gate = jax.nn.sigmoid(gate_pre)
    activated = gate_pre * sigmoid_gate
    hidden = (activated * up_pre).astype(jnp.bfloat16)
    out_rows = jnp.einsum(
        "erf,efd->erd", hidden, full_down, preferred_element_type=jnp.float32
    ).astype(jnp.bfloat16)
    d_hidden = jnp.einsum("erd,efd->erf", rows_cot, full_down, preferred_element_type=jnp.float32)
    d_gate = (d_hidden * up_pre * (sigmoid_gate + activated * (1.0 - sigmoid_gate))).astype(
        jnp.bfloat16
    )
    d_up = (d_hidden * activated).astype(jnp.bfloat16)
    d_both = jnp.concatenate([d_gate, d_up], axis=-1)
    dx_rows = jnp.einsum(
        "erg,egd->erd", d_both, gate_up, preferred_element_type=jnp.float32
    ).astype(jnp.bfloat16)
    part_down = jnp.einsum("erf,erd->efd", hidden, rows_cot, preferred_element_type=jnp.float32)
    part_both = jnp.einsum("erg,erd->egd", d_both, rows_in, preferred_element_type=jnp.float32)
    part_gate = part_both[:, :full_hidden]
    part_up = part_both[:, full_hidden:]

    back = jnp.stack([out_rows, dx_rows], axis=1)
    back = back.reshape(local_experts, 2, n_in, 2 * slots, width).transpose(2, 0, 1, 3, 4)
    back = back.reshape(half_experts, 2, 2 * slots, width)
    back = lax.all_to_all(back, "inner", split_axis=0, concat_axis=0, tiled=True)

    parts = jnp.concatenate([part_gate, part_up, part_down], axis=0)
    summed = parts[:, :hidden_part]
    for d in range(1, n_dp):
        block = parts[:, d * hidden_part : (d + 1) * hidden_part].astype(jnp.bfloat16)
        summed = summed + shifted(block, "dp", n_dp, -d).astype(jnp.float32)
    summed = summed.astype(jnp.bfloat16)
    grad_gate_w = summed[:local_experts]
    grad_up_w = summed[local_experts : 2 * local_experts]
    grad_down_w = summed[2 * local_experts :]

    out_part = back[:, 0].reshape(2 * half_rows, width)
    dx_part = back[:, 1].reshape(2 * half_rows, width)
    hit = dest[:, :, None] == jnp.arange(2 * half_rows, dtype=jnp.int32)[None, None, :]
    weight = jnp.sum(jnp.where(hit, all_gates[:, :, None], 0.0), axis=1)
    ones = jnp.sum(hit.astype(jnp.float32), axis=1).astype(jnp.bfloat16)
    layer = jnp.dot(in_three(weight), out_part, preferred_element_type=jnp.float32)
    n_all = 2 * tok_rows
    layer = layer[:n_all] + layer[n_all : 2 * n_all] + layer[2 * n_all :]
    grads = jnp.dot(ones, dx_part, preferred_element_type=jnp.float32)
    scores = jnp.dot(all_rows[:, width:], out_part.T, preferred_element_type=jnp.float32)
    gg = jnp.sum(jnp.where(hit, scores[:, None, :], 0.0), axis=2)

    returned = shifted(
        jnp.concatenate([layer[tok_rows:], grads[tok_rows:]], axis=1).astype(jnp.bfloat16),
        "half",
        2,
        1,
    )
    returned_gg = shifted(gg[tok_rows:], "half", 2, 1)
    layer_out = (layer[:tok_rows] + returned[:, :width].astype(jnp.float32)).astype(jnp.bfloat16)
    grad_tokens = (grads[:tok_rows] + returned[:, width:].astype(jnp.float32)).astype(jnp.bfloat16)
    grad_gates = gg[:tok_rows] + returned_gg
    return (layer_out, grad_tokens, grad_gates, grad_gate_w, grad_up_w, grad_down_w)


def solution(mesh):
    n_expert = mesh.shape["expert"]
    n_dp = mesh.shape["dp"]
    devices = np.asarray(mesh.devices).reshape(2, n_expert // 2, n_dp)
    split = Mesh(devices, ("half", "inner", "dp"))
    rows = P(("half", "inner", "dp"), None)
    weights = P(("half", "inner"), "dp", None)
    return jax.shard_map(
        on_device,
        mesh=split,
        in_specs=(rows, rows, rows, rows, P(), weights, weights, weights),
        out_specs=(rows, rows, rows, weights, weights, weights),
        check_vma=False,
    )
```

```python
import jax
import jax.numpy as jnp
import numpy as np
from jax import lax
from jax.sharding import Mesh
from jax.sharding import PartitionSpec as P


def shifted(value, axis, count, shift):
    return lax.ppermute(value, axis, [(j, (j + shift) % count) for j in range(count)])


def in_three(value):
    first = value.astype(jnp.bfloat16)
    rest = value - first.astype(jnp.float32)
    second = rest.astype(jnp.bfloat16)
    third = (rest - second.astype(jnp.float32)).astype(jnp.bfloat16)
    return jnp.concatenate([first, second, third], axis=0)


def on_device(tokens, cotangent, expert_ids, gate_vals, capacity, w_gate, w_up, w_down):
    tok_rows, width = tokens.shape
    top_count = expert_ids.shape[1]
    experts = capacity.shape[0]
    local_experts, hidden_part, _ = w_gate.shape
    slots = max(2, (5 * tok_rows * top_count + 4 * experts - 1) // (4 * experts))
    n_in = lax.axis_size("inner")
    n_dp = lax.axis_size("dp")
    half = lax.axis_index("half")
    inner = lax.axis_index("inner")
    source = half * n_in + inner
    n_src = 2 * n_in
    half_experts = n_in * local_experts
    half_rows = half_experts * slots

    weights = jnp.concatenate([w_gate, w_up, w_down], axis=0)
    pieces = [weights] + [shifted(weights, "dp", n_dp, d) for d in range(1, n_dp)]

    both_rows = jnp.concatenate([tokens, cotangent], axis=1)
    partner_rows = shifted(both_rows, "half", 2, 1)
    partner_gates = shifted(gate_vals, "half", 2, 1)

    flat_ids = expert_ids.reshape(-1)
    one_hot = (flat_ids[:, None] == jnp.arange(experts, dtype=jnp.int32)[None, :]).astype(jnp.int32)
    running = jnp.cumsum(one_hot, axis=0)
    local_rank = jnp.sum(running * one_hot, axis=1) - 1
    counts = running[-1]
    count_rows = jnp.where(jnp.arange(n_src, dtype=jnp.int32)[:, None] == source, counts[None, :], 0)
    all_counts = lax.psum(count_rows, ("half", "inner"))
    code = (flat_ids * slots + local_rank).reshape(tok_rows, top_count)
    partner_code = shifted(code, "half", 2, 1)

    all_rows = jnp.concatenate([both_rows, partner_rows], axis=0)
    all_gates = jnp.concatenate([gate_vals, partner_gates], axis=0)
    all_code = jnp.concatenate([code, partner_code], axis=0)
    local = all_code // slots - half * half_experts
    inside = (local >= 0) & (local < half_experts)
    side = (jnp.arange(2 * tok_rows, dtype=jnp.int32) >= tok_rows).astype(jnp.int32)[:, None]
    dest = jnp.where(inside, (local * 2 + side) * slots + all_code % slots, 2 * half_rows)

    slot_ids = jnp.arange(2 * half_rows, dtype=jnp.int32)[:, None, None]
    lands = dest[None, :, :] == slot_ids
    pick = jnp.any(lands, axis=2).astype(jnp.bfloat16)
    slot_gate = jnp.sum(jnp.where(lands, all_gates[None, :, :], 0.0), axis=(1, 2))
    picked = jnp.dot(pick, all_rows, preferred_element_type=jnp.float32)
    lane = jnp.arange(2 * width, dtype=jnp.int32)[None, :]
    scale = jnp.where(lane < width, 1.0, slot_gate[:, None])
    send = (picked * scale).astype(jnp.bfloat16).reshape(half_experts, 2 * slots, 2 * width)
    got = lax.all_to_all(send, "inner", split_axis=0, concat_axis=0, tiled=True)
    got = got.reshape(n_in, local_experts, 2, slots, 2 * width)

    earlier = jnp.cumsum(all_counts, axis=0) - all_counts
    holders = jnp.arange(n_in, dtype=jnp.int32)[:, None]
    halves = jnp.stack([half, 1 - half])[None, :]
    sources = halves * n_in + holders
    mine = (half * n_in + inner) * local_experts + jnp.arange(local_experts, dtype=jnp.int32)
    before = earlier[sources][:, :, mine].transpose(0, 2, 1)
    ranks = jnp.arange(slots, dtype=jnp.int32)
    keep = before[..., None] + ranks < capacity[mine][None, :, None, None]
    got = jnp.where(keep[..., None], got, jnp.zeros((), got.dtype))
    if local_experts == 1:
        got = got.reshape(1, n_in * 2 * slots, 2 * width)
    else:
        got = got.transpose(1, 0, 2, 3, 4).reshape(local_experts, n_in * 2 * slots, 2 * width)
    rows_in = got[:, :, :width]
    rows_cot = got[:, :, width:]

    full = jnp.concatenate(pieces, axis=1)
    full_down = full[2 * local_experts :]

    full_hidden = full.shape[1]
    if local_experts == 1:
        gate_up = full[:2].reshape(1, 2 * full_hidden, width)
    else:
        gate_up = full[: 2 * local_experts].reshape(2, local_experts, full_hidden, width)
        gate_up = gate_up.transpose(1, 0, 2, 3).reshape(local_experts, 2 * full_hidden, width)
    both_pre = jnp.einsum("erd,egd->erg", rows_in, gate_up, preferred_element_type=jnp.float32)
    gate_pre = both_pre[..., :full_hidden]
    up_pre = both_pre[..., full_hidden:]
    sigmoid_gate = jax.nn.sigmoid(gate_pre)
    activated = gate_pre * sigmoid_gate
    hidden = (activated * up_pre).astype(jnp.bfloat16)
    out_rows = jnp.einsum(
        "erf,efd->erd", hidden, full_down, preferred_element_type=jnp.float32
    ).astype(jnp.bfloat16)
    d_hidden = jnp.einsum("erd,efd->erf", rows_cot, full_down, preferred_element_type=jnp.float32)
    d_gate = (d_hidden * up_pre * (sigmoid_gate + activated * (1.0 - sigmoid_gate))).astype(
        jnp.bfloat16
    )
    d_up = (d_hidden * activated).astype(jnp.bfloat16)
    d_both = jnp.concatenate([d_gate, d_up], axis=-1)
    dx_rows = jnp.einsum(
        "erg,egd->erd", d_both, gate_up, preferred_element_type=jnp.float32
    ).astype(jnp.bfloat16)
    part_down = jnp.einsum("erf,erd->efd", hidden, rows_cot, preferred_element_type=jnp.float32)
    part_both = jnp.einsum("erg,erd->egd", d_both, rows_in, preferred_element_type=jnp.float32)
    part_gate = part_both[:, :full_hidden]
    part_up = part_both[:, full_hidden:]

    back = jnp.stack([out_rows, dx_rows], axis=1)
    back = back.reshape(local_experts, 2, n_in, 2 * slots, width).transpose(2, 0, 1, 3, 4)
    back = back.reshape(half_experts, 2, 2 * slots, width)
    back = lax.all_to_all(back, "inner", split_axis=0, concat_axis=0, tiled=True)

    parts = jnp.concatenate([part_gate, part_up, part_down], axis=0)
    summed = parts[:, :hidden_part]
    for d in range(1, n_dp):
        block = parts[:, d * hidden_part : (d + 1) * hidden_part].astype(jnp.bfloat16)
        summed = summed + shifted(block, "dp", n_dp, -d).astype(jnp.float32)
    summed = summed.astype(jnp.bfloat16)
    grad_gate_w = summed[:local_experts]
    grad_up_w = summed[local_experts : 2 * local_experts]
    grad_down_w = summed[2 * local_experts :]

    out_part = back[:, 0].reshape(2 * half_rows, width)
    dx_part = back[:, 1].reshape(2 * half_rows, width)
    columns = jnp.arange(2 * half_rows, dtype=jnp.int32)

    def combine(which):
        rows = slice(which * tok_rows, (which + 1) * tok_rows)
        hit = dest[rows][:, :, None] == columns[None, None, :]
        weight = jnp.sum(jnp.where(hit, all_gates[rows][:, :, None], 0.0), axis=1)
        ones = jnp.sum(hit.astype(jnp.float32), axis=1).astype(jnp.bfloat16)
        layer = jnp.dot(in_three(weight), out_part, preferred_element_type=jnp.float32)
        layer = layer[:tok_rows] + layer[tok_rows : 2 * tok_rows] + layer[2 * tok_rows :]
        grads = jnp.dot(ones, dx_part, preferred_element_type=jnp.float32)
        scores = jnp.dot(all_rows[rows, width:], out_part.T, preferred_element_type=jnp.float32)
        gg = jnp.sum(jnp.where(hit, scores[:, None, :], 0.0), axis=2)
        return layer, grads, gg

    partner_layer, partner_grads, partner_gg = combine(1)
    returned = shifted(
        jnp.concatenate([partner_layer, partner_grads], axis=1).astype(jnp.bfloat16), "half", 2, 1
    )
    returned_gg = shifted(partner_gg, "half", 2, 1)
    own_layer, own_grads, own_gg = combine(0)
    layer_out = (own_layer + returned[:, :width].astype(jnp.float32)).astype(jnp.bfloat16)
    grad_tokens = (own_grads + returned[:, width:].astype(jnp.float32)).astype(jnp.bfloat16)
    grad_gates = own_gg + returned_gg
    return (layer_out, grad_tokens, grad_gates, grad_gate_w, grad_up_w, grad_down_w)


def solution(mesh):
    n_expert = mesh.shape["expert"]
    n_dp = mesh.shape["dp"]
    devices = np.asarray(mesh.devices).reshape(2, n_expert // 2, n_dp)
    split = Mesh(devices, ("half", "inner", "dp"))
    rows = P(("half", "inner", "dp"), None)
    weights = P(("half", "inner"), "dp", None)
    return jax.shard_map(
        on_device,
        mesh=split,
        in_specs=(rows, rows, rows, rows, P(), weights, weights, weights),
        out_specs=(rows, rows, rows, weights, weights, weights),
        check_vma=False,
    )
```

```python
import jax
import jax.numpy as jnp
import numpy as np
from jax import lax
from jax.sharding import Mesh
from jax.sharding import PartitionSpec as P


def shifted(value, axis, count, shift):
    return lax.ppermute(value, axis, [(j, (j + shift) % count) for j in range(count)])


def in_three(value):
    first = value.astype(jnp.bfloat16)
    rest = value - first.astype(jnp.float32)
    second = rest.astype(jnp.bfloat16)
    third = (rest - second.astype(jnp.float32)).astype(jnp.bfloat16)
    return jnp.concatenate([first, second, third], axis=0)


def on_device(tokens, cotangent, expert_ids, gate_vals, capacity, w_gate, w_up, w_down):
    tok_rows, width = tokens.shape
    top_count = expert_ids.shape[1]
    experts = capacity.shape[0]
    local_experts, hidden_part, _ = w_gate.shape
    slots = max(2, (5 * tok_rows * top_count + 4 * experts - 1) // (4 * experts))
    n_in = lax.axis_size("inner")
    n_dp = lax.axis_size("dp")
    half = lax.axis_index("half")
    inner = lax.axis_index("inner")
    source = half * n_in + inner
    n_src = 2 * n_in
    half_experts = n_in * local_experts
    half_rows = half_experts * slots

    weights = jnp.concatenate([w_gate, w_up, w_down], axis=0)
    pieces = [weights] + [shifted(weights, "dp", n_dp, d) for d in range(1, n_dp)]

    both_rows = jnp.concatenate([tokens, cotangent], axis=1)
    partner_rows = shifted(both_rows, "half", 2, 1)
    partner_gates = shifted(gate_vals, "half", 2, 1)

    flat_ids = expert_ids.reshape(-1)
    one_hot = (flat_ids[:, None] == jnp.arange(experts, dtype=jnp.int32)[None, :]).astype(jnp.int32)
    running = jnp.cumsum(one_hot, axis=0)
    local_rank = jnp.sum(running * one_hot, axis=1) - 1
    counts = running[-1]
    count_rows = jnp.where(jnp.arange(n_src, dtype=jnp.int32)[:, None] == source, counts[None, :], 0)
    all_counts = lax.psum(count_rows, ("half", "inner"))
    code = (flat_ids * slots + local_rank).reshape(tok_rows, top_count)
    partner_code = shifted(code, "half", 2, 1)

    all_gates = jnp.concatenate([gate_vals, partner_gates], axis=0)
    all_code = jnp.concatenate([code, partner_code], axis=0)
    local = all_code // slots - half * half_experts
    inside = (local >= 0) & (local < half_experts)
    side = (jnp.arange(2 * tok_rows, dtype=jnp.int32) >= tok_rows).astype(jnp.int32)[:, None]
    dest = jnp.where(inside, (local * 2 + side) * slots + all_code % slots, 2 * half_rows)

    slot_ids = jnp.arange(2 * half_rows, dtype=jnp.int32)[:, None, None]
    lands = dest[None, :, :] == slot_ids
    slot_gate = jnp.sum(jnp.where(lands, all_gates[None, :, :], 0.0), axis=(1, 2))
    picked = jnp.dot(
        jnp.any(lands[:, :tok_rows], axis=2).astype(jnp.bfloat16),
        both_rows,
        preferred_element_type=jnp.float32,
    ) + jnp.dot(
        jnp.any(lands[:, tok_rows:], axis=2).astype(jnp.bfloat16),
        partner_rows,
        preferred_element_type=jnp.float32,
    )
    lane = jnp.arange(2 * width, dtype=jnp.int32)[None, :]
    scale = jnp.where(lane < width, 1.0, slot_gate[:, None])
    send = (picked * scale).astype(jnp.bfloat16).reshape(half_experts, 2 * slots, 2 * width)
    got = lax.all_to_all(send, "inner", split_axis=0, concat_axis=0, tiled=True)
    got = got.reshape(n_in, local_experts, 2, slots, 2 * width)

    earlier = jnp.cumsum(all_counts, axis=0) - all_counts
    holders = jnp.arange(n_in, dtype=jnp.int32)[:, None]
    halves = jnp.stack([half, 1 - half])[None, :]
    sources = halves * n_in + holders
    mine = (half * n_in + inner) * local_experts + jnp.arange(local_experts, dtype=jnp.int32)
    before = earlier[sources][:, :, mine].transpose(0, 2, 1)
    ranks = jnp.arange(slots, dtype=jnp.int32)
    keep = before[..., None] + ranks < capacity[mine][None, :, None, None]
    got = jnp.where(keep[..., None], got, jnp.zeros((), got.dtype))
    if local_experts == 1:
        got = got.reshape(1, n_in * 2 * slots, 2 * width)
    else:
        got = got.transpose(1, 0, 2, 3, 4).reshape(local_experts, n_in * 2 * slots, 2 * width)
    rows_in = got[:, :, :width]
    rows_cot = got[:, :, width:]

    full = jnp.concatenate(pieces, axis=1)
    full_down = full[2 * local_experts :]

    full_hidden = full.shape[1]
    if local_experts == 1:
        gate_up = full[:2].reshape(1, 2 * full_hidden, width)
    else:
        gate_up = full[: 2 * local_experts].reshape(2, local_experts, full_hidden, width)
        gate_up = gate_up.transpose(1, 0, 2, 3).reshape(local_experts, 2 * full_hidden, width)
    both_pre = jnp.einsum("erd,egd->erg", rows_in, gate_up, preferred_element_type=jnp.float32)
    gate_pre = both_pre[..., :full_hidden]
    up_pre = both_pre[..., full_hidden:]
    sigmoid_gate = jax.nn.sigmoid(gate_pre)
    activated = gate_pre * sigmoid_gate
    hidden = (activated * up_pre).astype(jnp.bfloat16)
    out_rows = jnp.einsum(
        "erf,efd->erd", hidden, full_down, preferred_element_type=jnp.float32
    ).astype(jnp.bfloat16)
    d_hidden = jnp.einsum("erd,efd->erf", rows_cot, full_down, preferred_element_type=jnp.float32)
    d_gate = (d_hidden * up_pre * (sigmoid_gate + activated * (1.0 - sigmoid_gate))).astype(
        jnp.bfloat16
    )
    d_up = (d_hidden * activated).astype(jnp.bfloat16)
    d_both = jnp.concatenate([d_gate, d_up], axis=-1)
    dx_rows = jnp.einsum(
        "erg,egd->erd", d_both, gate_up, preferred_element_type=jnp.float32
    ).astype(jnp.bfloat16)
    part_down = jnp.einsum("erf,erd->efd", hidden, rows_cot, preferred_element_type=jnp.float32)
    part_both = jnp.einsum("erg,erd->egd", d_both, rows_in, preferred_element_type=jnp.float32)
    part_gate = part_both[:, :full_hidden]
    part_up = part_both[:, full_hidden:]

    back = jnp.stack([out_rows, dx_rows], axis=1)
    back = back.reshape(local_experts, 2, n_in, 2 * slots, width).transpose(2, 0, 1, 3, 4)
    back = back.reshape(half_experts, 2, 2 * slots, width)
    back = lax.all_to_all(back, "inner", split_axis=0, concat_axis=0, tiled=True)

    parts = jnp.concatenate([part_gate, part_up, part_down], axis=0)
    summed = parts[:, :hidden_part]
    for d in range(1, n_dp):
        block = parts[:, d * hidden_part : (d + 1) * hidden_part].astype(jnp.bfloat16)
        summed = summed + shifted(block, "dp", n_dp, -d).astype(jnp.float32)
    summed = summed.astype(jnp.bfloat16)
    grad_gate_w = summed[:local_experts]
    grad_up_w = summed[local_experts : 2 * local_experts]
    grad_down_w = summed[2 * local_experts :]

    out_part = back[:, 0].reshape(2 * half_rows, width)
    dx_part = back[:, 1].reshape(2 * half_rows, width)
    columns = jnp.arange(2 * half_rows, dtype=jnp.int32)

    def combine(which):
        rows = slice(which * tok_rows, (which + 1) * tok_rows)
        hit = dest[rows][:, :, None] == columns[None, None, :]
        weight = jnp.sum(jnp.where(hit, all_gates[rows][:, :, None], 0.0), axis=1)
        ones = jnp.sum(hit.astype(jnp.float32), axis=1).astype(jnp.bfloat16)
        layer = jnp.dot(in_three(weight), out_part, preferred_element_type=jnp.float32)
        layer = layer[:tok_rows] + layer[tok_rows : 2 * tok_rows] + layer[2 * tok_rows :]
        grads = jnp.dot(ones, dx_part, preferred_element_type=jnp.float32)
        cot_rows = (both_rows if which == 0 else partner_rows)[:, width:]
        scores = jnp.dot(cot_rows, out_part.T, preferred_element_type=jnp.float32)
        gg = jnp.sum(jnp.where(hit, scores[:, None, :], 0.0), axis=2)
        return layer, grads, gg

    partner_layer, partner_grads, partner_gg = combine(1)
    returned = shifted(
        jnp.concatenate([partner_layer, partner_grads], axis=1).astype(jnp.bfloat16), "half", 2, 1
    )
    returned_gg = shifted(partner_gg, "half", 2, 1)
    own_layer, own_grads, own_gg = combine(0)
    layer_out = (own_layer + returned[:, :width].astype(jnp.float32)).astype(jnp.bfloat16)
    grad_tokens = (own_grads + returned[:, width:].astype(jnp.float32)).astype(jnp.bfloat16)
    grad_gates = own_gg + returned_gg
    return (layer_out, grad_tokens, grad_gates, grad_gate_w, grad_up_w, grad_down_w)


def solution(mesh):
    n_expert = mesh.shape["expert"]
    n_dp = mesh.shape["dp"]
    devices = np.asarray(mesh.devices).reshape(2, n_expert // 2, n_dp)
    split = Mesh(devices, ("half", "inner", "dp"))
    rows = P(("half", "inner", "dp"), None)
    weights = P(("half", "inner"), "dp", None)
    return jax.shard_map(
        on_device,
        mesh=split,
        in_specs=(rows, rows, rows, rows, P(), weights, weights, weights),
        out_specs=(rows, rows, rows, weights, weights, weights),
        check_vma=False,
    )
```

```python
import jax
import jax.numpy as jnp
import numpy as np
from jax import lax
from jax.sharding import Mesh
from jax.sharding import PartitionSpec as P


def shifted(value, axis, count, shift):
    return lax.ppermute(value, axis, [(j, (j + shift) % count) for j in range(count)])


def in_three(value):
    first = value.astype(jnp.bfloat16)
    rest = value - first.astype(jnp.float32)
    second = rest.astype(jnp.bfloat16)
    third = (rest - second.astype(jnp.float32)).astype(jnp.bfloat16)
    return jnp.concatenate([first, second, third], axis=0)


def on_device(tokens, cotangent, expert_ids, gate_vals, capacity, w_gate, w_up, w_down):
    tok_rows, width = tokens.shape
    top_count = expert_ids.shape[1]
    experts = capacity.shape[0]
    local_experts, hidden_part, _ = w_gate.shape
    slots = max(2, (5 * tok_rows * top_count + 4 * experts - 1) // (4 * experts))
    n_in = lax.axis_size("inner")
    n_dp = lax.axis_size("dp")
    half = lax.axis_index("half")
    inner = lax.axis_index("inner")
    source = half * n_in + inner
    n_src = 2 * n_in
    half_experts = n_in * local_experts
    half_rows = half_experts * slots

    weights = jnp.concatenate([w_gate, w_up, w_down], axis=0)
    pieces = [weights] + [shifted(weights, "dp", n_dp, d) for d in range(1, n_dp)]

    both_rows = jnp.concatenate([tokens, cotangent], axis=1)
    partner_rows = shifted(both_rows, "half", 2, 1)
    partner_gates = shifted(gate_vals, "half", 2, 1)

    flat_ids = expert_ids.reshape(-1)
    one_hot = (flat_ids[:, None] == jnp.arange(experts, dtype=jnp.int32)[None, :]).astype(jnp.int32)
    running = jnp.cumsum(one_hot, axis=0)
    local_rank = jnp.sum(running * one_hot, axis=1) - 1
    counts = running[-1]
    count_rows = jnp.where(jnp.arange(n_src, dtype=jnp.int32)[:, None] == source, counts[None, :], 0)
    all_counts = lax.psum(count_rows, ("half", "inner"))
    code = (flat_ids * slots + local_rank).reshape(tok_rows, top_count)
    partner_code = shifted(code, "half", 2, 1)

    all_rows = jnp.concatenate([both_rows, partner_rows], axis=0)
    all_gates = jnp.concatenate([gate_vals, partner_gates], axis=0)
    all_code = jnp.concatenate([code, partner_code], axis=0)
    local = all_code // slots - half * half_experts
    inside = (local >= 0) & (local < half_experts)
    side = (jnp.arange(2 * tok_rows, dtype=jnp.int32) >= tok_rows).astype(jnp.int32)[:, None]
    dest = jnp.where(inside, (local * 2 + side) * slots + all_code % slots, 2 * half_rows)

    slot_ids = jnp.arange(2 * half_rows, dtype=jnp.int32)[:, None, None]
    lands = dest[None, :, :] == slot_ids
    pick = jnp.any(lands, axis=2).astype(jnp.bfloat16)
    slot_gate = jnp.sum(jnp.where(lands, all_gates[None, :, :], 0.0), axis=(1, 2))
    picked = jnp.dot(pick, all_rows, preferred_element_type=jnp.float32)
    lane = jnp.arange(2 * width, dtype=jnp.int32)[None, :]
    scale = jnp.where(lane < width, 1.0, slot_gate[:, None])
    send = (picked * scale).astype(jnp.bfloat16).reshape(half_experts, 2 * slots, 2 * width)
    got = lax.all_to_all(send, "inner", split_axis=0, concat_axis=0, tiled=True)
    got = got.reshape(n_in, local_experts, 2, slots, 2 * width)

    earlier = jnp.cumsum(all_counts, axis=0) - all_counts
    holders = jnp.arange(n_in, dtype=jnp.int32)[:, None]
    halves = jnp.stack([half, 1 - half])[None, :]
    sources = halves * n_in + holders
    mine = (half * n_in + inner) * local_experts + jnp.arange(local_experts, dtype=jnp.int32)
    before = earlier[sources][:, :, mine].transpose(0, 2, 1)
    ranks = jnp.arange(slots, dtype=jnp.int32)
    keep = before[..., None] + ranks < capacity[mine][None, :, None, None]
    if local_experts == 1:
        got = got.reshape(1, n_in * 2 * slots, 2 * width)
        keep = keep.reshape(1, n_in * 2 * slots, 1)
    else:
        got = got.transpose(1, 0, 2, 3, 4).reshape(local_experts, n_in * 2 * slots, 2 * width)
        keep = keep.transpose(1, 0, 2, 3).reshape(local_experts, n_in * 2 * slots, 1)
    rows_in = got[:, :, :width]
    rows_cot = got[:, :, width:]

    full = jnp.concatenate(pieces, axis=1)
    full_down = full[2 * local_experts :]

    full_hidden = full.shape[1]
    if local_experts == 1:
        gate_up = full[:2].reshape(1, 2 * full_hidden, width)
    else:
        gate_up = full[: 2 * local_experts].reshape(2, local_experts, full_hidden, width)
        gate_up = gate_up.transpose(1, 0, 2, 3).reshape(local_experts, 2 * full_hidden, width)
    both_pre = jnp.einsum("erd,egd->erg", rows_in, gate_up, preferred_element_type=jnp.float32)
    gate_pre = both_pre[..., :full_hidden]
    up_pre = both_pre[..., full_hidden:]
    sigmoid_gate = jax.nn.sigmoid(gate_pre)
    activated = gate_pre * sigmoid_gate
    hidden = jnp.where(keep, activated * up_pre, 0.0).astype(jnp.bfloat16)
    out_rows = jnp.einsum(
        "erf,efd->erd", hidden, full_down, preferred_element_type=jnp.float32
    ).astype(jnp.bfloat16)
    d_hidden = jnp.einsum("erd,efd->erf", rows_cot, full_down, preferred_element_type=jnp.float32)
    d_gate = (d_hidden * up_pre * (sigmoid_gate + activated * (1.0 - sigmoid_gate))).astype(
        jnp.bfloat16
    )
    d_up = (d_hidden * activated).astype(jnp.bfloat16)
    d_both = jnp.where(keep, jnp.concatenate([d_gate, d_up], axis=-1), jnp.zeros((), jnp.bfloat16))
    dx_rows = jnp.einsum(
        "erg,egd->erd", d_both, gate_up, preferred_element_type=jnp.float32
    ).astype(jnp.bfloat16)
    part_down = jnp.einsum("erf,erd->efd", hidden, rows_cot, preferred_element_type=jnp.float32)
    part_both = jnp.einsum("erg,erd->egd", d_both, rows_in, preferred_element_type=jnp.float32)
    part_gate = part_both[:, :full_hidden]
    part_up = part_both[:, full_hidden:]

    back = jnp.stack([out_rows, dx_rows], axis=1)
    back = back.reshape(local_experts, 2, n_in, 2 * slots, width).transpose(2, 0, 1, 3, 4)
    back = back.reshape(half_experts, 2, 2 * slots, width)
    back = lax.all_to_all(back, "inner", split_axis=0, concat_axis=0, tiled=True)

    parts = jnp.concatenate([part_gate, part_up, part_down], axis=0)
    summed = parts[:, :hidden_part]
    for d in range(1, n_dp):
        block = parts[:, d * hidden_part : (d + 1) * hidden_part].astype(jnp.bfloat16)
        summed = summed + shifted(block, "dp", n_dp, -d).astype(jnp.float32)
    summed = summed.astype(jnp.bfloat16)
    grad_gate_w = summed[:local_experts]
    grad_up_w = summed[local_experts : 2 * local_experts]
    grad_down_w = summed[2 * local_experts :]

    out_part = back[:, 0].reshape(2 * half_rows, width)
    dx_part = back[:, 1].reshape(2 * half_rows, width)
    columns = jnp.arange(2 * half_rows, dtype=jnp.int32)

    def combine(which):
        rows = slice(which * tok_rows, (which + 1) * tok_rows)
        hit = dest[rows][:, :, None] == columns[None, None, :]
        weight = jnp.sum(jnp.where(hit, all_gates[rows][:, :, None], 0.0), axis=1)
        ones = jnp.sum(hit.astype(jnp.float32), axis=1).astype(jnp.bfloat16)
        layer = jnp.dot(in_three(weight), out_part, preferred_element_type=jnp.float32)
        layer = layer[:tok_rows] + layer[tok_rows : 2 * tok_rows] + layer[2 * tok_rows :]
        grads = jnp.dot(ones, dx_part, preferred_element_type=jnp.float32)
        scores = jnp.dot(all_rows[rows, width:], out_part.T, preferred_element_type=jnp.float32)
        gg = jnp.sum(jnp.where(hit, scores[:, None, :], 0.0), axis=2)
        return layer, grads, gg

    partner_layer, partner_grads, partner_gg = combine(1)
    returned = shifted(
        jnp.concatenate([partner_layer, partner_grads], axis=1).astype(jnp.bfloat16), "half", 2, 1
    )
    returned_gg = shifted(partner_gg, "half", 2, 1)
    own_layer, own_grads, own_gg = combine(0)
    layer_out = (own_layer + returned[:, :width].astype(jnp.float32)).astype(jnp.bfloat16)
    grad_tokens = (own_grads + returned[:, width:].astype(jnp.float32)).astype(jnp.bfloat16)
    grad_gates = own_gg + returned_gg
    return (layer_out, grad_tokens, grad_gates, grad_gate_w, grad_up_w, grad_down_w)


def solution(mesh):
    n_expert = mesh.shape["expert"]
    n_dp = mesh.shape["dp"]
    devices = np.asarray(mesh.devices).reshape(2, n_expert // 2, n_dp)
    split = Mesh(devices, ("half", "inner", "dp"))
    rows = P(("half", "inner", "dp"), None)
    weights = P(("half", "inner"), "dp", None)
    return jax.shard_map(
        on_device,
        mesh=split,
        in_specs=(rows, rows, rows, rows, P(), weights, weights, weights),
        out_specs=(rows, rows, rows, weights, weights, weights),
        check_vma=False,
    )
```
